32 devices in a mesh: space: 8 (over z, x), batch: 4 (over y, core).
Axes of the slice: x: 2, y: 2, z: 4, core: 2. Of those that a mesh axis runs over, the one named last changes fastest.
Arguments:
- owner: int32 [8, 2048, 1], P('batch', 'space'), may hold values from 0 to 7; in each aligned block of 256 rows (0 to 255, 256 to 511, ..., all dimensions but the last counted through in order) at most 128 rows name the same one
- offset: int32 [8, 2048], P('batch', 'space'), may hold values from 0 to 2047
- profile: float32 [8, 2048, 128], P('batch', 'space'), may hold values from -6 to 6
- diffusion: float32 [32, 512, 128], P('space'), may hold values from 0.04 to 0.16
- velocity: float32 [32, 512, 128], P('space'), may hold values from 0.05 to 0.3
Outputs:
- final_fields: float32 [8, 32, 512, 128], P('batch', 'space')
- gram: float32 [8, 8], replicated
The draws below stay inside these ranges and needn't reach their ends.
Inputs may be any that keep to these rules, and one draw needn't show every extreme that they name: In each aligned block of 256 rows of owner (one field's rows on one index of space), no value is named by more than 128 rows, a bound that some block reaches.
All inputs are finite; a program needn't handle non-finite values.
Results may differ from the reference program's by a relative error of at most 0.0042.
Values may be sent and summed in bfloat16 or wider, within the bound.
No kernel may reach another device: no remote copies, remote signals or barrier semaphores. Data moves between devices by JAX's collectives and lax.ppermute only.
A program may use at most 320 MiB of HBM per device.

```python
import math
import jax
import jax.numpy as jnp
import numpy as np

CX = 4
NY = 512
NZ = 128
STEPS = 2
ACT = 4
SENS = 4
ROWS_DEV = 256
FIELDS = 8
NX = 32
LOADS = 2048
CAP = 128
N_SPACE = 8


def touch_ends(array, key, smallest, largest):
    index_at = [jax.random.randint(jax.random.fold_in(key, axis), (), 0, length) for axis, length in enumerate(array.shape)]
    widest = array.shape.index(max(array.shape))
    beside = index_at[:widest] + [(index_at[widest] + 1) % array.shape[widest]] + index_at[widest + 1:]
    return array.at[tuple(index_at)].set(smallest).at[tuple(beside)].set(largest)


def steps_of(key, shape, cuts, low, largest):
    loudness = 1.0
    for axis_at, shards_of in cuts:
        heights = jax.random.uniform(jax.random.fold_in(jax.random.fold_in(key, 6), axis_at), (shards_of,), jnp.float32, low / len(cuts), largest / len(cuts))
        loudness = loudness * jnp.repeat(jnp.exp(heights), shape[axis_at] // shards_of).reshape((-1,) + (1,) * (len(shape) - 1 - axis_at))
    return loudness


def deal_out(key, own, number, rows, amount, top, bound, lean):
    ranking = jax.random.permutation(key, amount)
    crowded, common = shares(amount, rows * top, bound, lean, True), shares(amount, rows * top, bound, lean, False)
    places = jnp.arange(amount)

    def named(tallies, rotation):
        used = int((tallies > 0).sum())
        fixed = max(1, used // 4)
        moved = fixed + (places - fixed + rotation * (used - fixed)) % max(1, amount - fixed)
        return jnp.zeros((amount,), jnp.int32).at[ranking[jnp.where(places < fixed, places, moved)]].set(jnp.asarray(tallies, jnp.int32))

    tallies = jnp.where(number % 4 == 0, named(crowded, number // 4), named(common, number - number // 4 - 1))
    mixed = jax.random.permutation(jax.random.fold_in(own, 3), amount)
    giver, sink = mixed[0:amount // 2 * 2:2], mixed[1:amount // 2 * 2:2]
    room = jnp.minimum(tallies[giver] - 1, bound - tallies[sink]) // 2
    room = jnp.where((giver == ranking[0]) | (sink == ranking[0]) | (tallies[sink] == 0), 0, jnp.maximum(room, 0))
    moved = jax.random.randint(jax.random.fold_in(own, 4), (amount // 2,), 0, 1 << 20) % (room + 1)
    tallies = tallies.at[giver].add(-moved).at[sink].add(moved)
    labels = jnp.searchsorted(jnp.cumsum(tallies), jnp.arange(rows * top), side="right").astype(jnp.int32)
    grid = labels.reshape(top, rows).T
    grid = grid[jax.random.permutation(jax.random.fold_in(own, 1), rows)]
    rotation = jax.random.randint(jax.random.fold_in(own, 2), (rows, 1), 0, top)
    return jnp.take_along_axis(grid, (jnp.arange(top)[None, :] + rotation) % top, axis=1)


def shares(amount, total, limit, slope, full):
    weights = [(1 << 20) // math.isqrt(rank ** slope) + 1 for rank in range(1, amount + 1)]
    largest = limit if full else min(limit, max(-(-total // amount), total * weights[0] // sum(weights)))
    least = 1 if total - largest >= amount - 1 else 0
    holding, spare = [largest] + [least] * (amount - 1), total - largest - least * (amount - 1)
    while spare > 0:
        candidates = [i for i in range(1, amount) if holding[i] < largest] or [i for i in range(1, amount) if holding[i] < limit]
        whole, budget = sum([weights[i] for i in candidates]), spare
        for i in candidates:
            more = min(limit - holding[i], max(1, budget * weights[i] // whole), spare)
            holding[i] = holding[i] + more
            spare = spare - more
    return np.array(holding)


def bell_draw(own_key, extent, deviation, most, shards=(), held_as=jnp.bfloat16):
    level = steps_of(own_key, extent, shards, -0.22, 0.18) if shards else 1.0
    values = jax.random.normal(own_key, extent, jnp.float32) * deviation * level
    return jnp.minimum(jnp.maximum(values, -most), most).astype(held_as)


def setup_inputs(seed: int = 0) -> dict:
    seeds = jax.random.split(jax.random.key(seed), 6)
    owner_keys = jax.random.split(jax.random.fold_in(seeds[0], 1), FIELDS * LOADS // ROWS_DEV)
    owner_turns = jax.random.permutation(jax.random.fold_in(seeds[0], 3), FIELDS * LOADS // ROWS_DEV)
    owner = jax.vmap(lambda own, number: deal_out(jax.random.fold_in(seeds[0], 2), own, number, ROWS_DEV, N_SPACE, 1, CAP, 2))(owner_keys, owner_turns).reshape((FIELDS, LOADS, 1))
    offset = touch_ends(jax.random.randint(seeds[1], (FIELDS, LOADS), 0, CX * NY), jax.random.fold_in(seeds[1], 1), 0, (CX * NY) - 1).astype(jnp.int32)
    profile = bell_draw(seeds[2], (FIELDS, LOADS, NZ), 1.0, 6.0, ((0, 4), (1, 8)), jnp.float32)
    diffusion = jnp.clip(jnp.exp(math.log(0.16) - 1.3862944 * jax.random.uniform(seeds[3], (NX, NY, NZ), jnp.float32) ** steps_of(seeds[3], (NX, NY, NZ), ((0, 8),), -0.2, 0.2)), 0.04, 0.16)
    velocity = jnp.clip(0.05 + 0.25 * jax.random.uniform(seeds[4], (NX, NY, NZ), jnp.float32) ** steps_of(seeds[4], (NX, NY, NZ), ((0, 8),), -0.2, 0.2), 0.05, 0.3)
    return {"owner": owner, "offset": offset, "profile": profile, "diffusion": diffusion, "velocity": velocity}


def laplace(u):
    padded = jnp.pad(u, ((0, 0), (0, 0), (0, 0), (1, 1)))
    total = jnp.roll(u, -1, 1) + jnp.roll(u, 1, 1)
    total = total + jnp.roll(u, -1, 2) + jnp.roll(u, 1, 2)
    total = total + padded[..., 2:] + padded[..., :-2]
    return total - 6.0 * u

def central(u):
    return 0.5 * (jnp.roll(u, -1, 1) - jnp.roll(u, 1, 1))

def starting(owner, offset, profile):
    columns = (owner[..., 0] * (CX * NY) + offset).astype(jnp.int32)

    def single(col, prof):
        return jnp.zeros((NX * NY, NZ), jnp.float32).at[col].add(prof)
    return jax.vmap(single)(columns, profile).reshape(FIELDS, NX, NY, NZ)

def reference(owner, offset, profile, diffusion, velocity):
    fields = starting(owner, offset, profile)
    forward = fields[:ACT]
    adjoint = fields[ACT:]
    snaps_a = []
    snaps_s = []
    for step in range(STEPS):
        forward = forward + diffusion * laplace(forward) - velocity * central(forward)
        adjoint = adjoint + laplace(diffusion * adjoint) + central(velocity * adjoint)
        snaps_a.append(forward.astype(jnp.bfloat16).reshape(ACT, -1))
        snaps_s.append(adjoint.astype(jnp.bfloat16).reshape(SENS, -1))
    stack_a = jnp.concatenate(snaps_a, 0)
    stack_s = jnp.concatenate(snaps_s, 0)
    cross = jax.lax.dot_general(stack_s, stack_a, (((1,), (1,)), ((), ())), preferred_element_type=jnp.float32)
    gram = cross * (4.0 / math.sqrt(NX * NY * NZ))
    return (jnp.concatenate([forward, adjoint], 0), gram)
```

```python
import math

import jax
import jax.numpy as jnp
from jax import lax
from jax.sharding import PartitionSpec as P

STEPS = 2
ACT = 4
SENS = 4


def padded(value, axis, width, dim):
    peers, length = lax.axis_size(axis), value.shape[dim]
    up = [(i, (i + 1) % peers) for i in range(peers)]
    down = [(j, i) for i, j in up]
    last = lax.slice_in_dim(value, length - width, length, axis=dim)
    initial = lax.slice_in_dim(value, 0, width, axis=dim)
    before = lax.ppermute(last, axis, up)
    after = lax.ppermute(initial, axis, down)
    return jnp.concatenate([before, value, after], axis=dim)


def pieces(x):
    out, rest = [], x
    for _ in range(3):
        part = lax.reduce_precision(rest, exponent_bits=8, mantissa_bits=7)
        out.append(part.astype(jnp.bfloat16))
        rest = rest - part
    return out


def select(onehot, values):
    total = None
    for part in pieces(values):
        term = jnp.einsum("fmk,fkd->fmd", onehot, part, preferred_element_type=jnp.float32)
        total = term if total is None else total + term
    return total


def prepare(coef, adjoint):
    diff_c = coef[0]
    vel_c = coef[1]
    pre_lap = jnp.where(adjoint, diff_c, 1.0)
    post_lap = jnp.where(adjoint, 1.0, diff_c)
    pre_dx = jnp.where(adjoint, vel_c, 1.0)
    post_dx = jnp.where(adjoint, 1.0, -vel_c)
    return (pre_lap, post_lap, pre_dx, post_dx)


def advance(extended, weights):
    pre_lap, post_lap, pre_dx, post_dx = weights
    lifted = pre_lap * extended
    moved = pre_dx * extended
    middle = lifted[:, 1:-1]
    padded_z = jnp.pad(middle, ((0, 0), (0, 0), (0, 0), (1, 1)))
    total = lifted[:, 2:] + lifted[:, :-2]
    total = total + jnp.roll(middle, -1, 2) + jnp.roll(middle, 1, 2)
    total = total + padded_z[..., 2:] + padded_z[..., :-2]
    lapl = total - 6.0 * middle
    slope = 0.5 * (moved[:, 2:] - moved[:, :-2])
    return extended[:, 1:-1] + post_lap[1:-1] * lapl + post_dx[1:-1] * slope


def butterfly(value, axes):
    for axis in axes:
        n = lax.axis_size(axis)
        step = 1
        while step < n:
            value = value + lax.ppermute(value, axis, [(i, i ^ step) for i in range(n)])
            step *= 2
    return value


def body(owner, offset, profile, diffusion, velocity):
    count = lax.axis_size("space")
    fields_dev, rows_dev = offset.shape
    planes, span, depth = diffusion.shape
    cap = 4 * rows_dev // count
    slots = count * cap
    col_rows = -(-cap // depth)

    target = owner[..., 0]
    earlier = jnp.tril(jnp.ones((rows_dev, rows_dev), jnp.bool_), -1)
    same = target[:, :, None] == target[:, None, :]
    rank = jnp.sum(jnp.logical_and(same, earlier[None]), axis=2)
    slot = target * cap + rank
    hit = slot[:, None, :] == lax.broadcasted_iota(jnp.int32, (fields_dev, slots, rows_dev), 1)
    send_vals = select(hit.astype(jnp.bfloat16), profile)
    send_cols = jnp.sum(jnp.where(hit, offset[:, None, :], 0), axis=2).astype(jnp.float32)
    send_cols = jnp.pad(send_cols.reshape(fields_dev, count, cap), ((0, 0), (0, 0), (0, col_rows * depth - cap)))
    payload = jnp.concatenate(
        [send_vals.reshape(fields_dev, count, cap, depth), send_cols.reshape(fields_dev, count, col_rows, depth)],
        axis=2,
    )
    got = lax.all_to_all(payload, "space", split_axis=1, concat_axis=1, tiled=True)
    got_vals = got[:, :, :cap].reshape(fields_dev, slots, depth)
    got_cols = got[:, :, cap:].reshape(fields_dev, count, col_rows * depth)[:, :, :cap]
    got_cols = got_cols.reshape(fields_dev, slots).astype(jnp.int32)

    place = got_cols[:, None, :] == lax.broadcasted_iota(jnp.int32, (fields_dev, planes * span, slots), 1)
    state = select(place.astype(jnp.bfloat16), got_vals).reshape(fields_dev, planes, span, depth)

    adjoint = lax.axis_index("batch") >= lax.axis_size("batch") // 2
    coef = jnp.stack([diffusion, velocity])
    rim = padded(coef, "space", STEPS, 1)
    weights = prepare(rim, adjoint)
    extended = padded(state, "space", STEPS, 1)

    pieces_ = []

    def record(current):
        snap = current.astype(jnp.bfloat16).reshape(fields_dev, -1)
        pieces_.append(lax.all_to_all(snap, "batch", split_axis=1, concat_axis=0, tiled=True))

    for step in range(STEPS):
        extended = advance(extended, weights)
        weights = tuple(w[1:-1] for w in weights)
        width = STEPS - 1 - step
        record(extended[:, width:extended.shape[1] - width])
    state = extended
    mixed = jnp.stack(pieces_)
    actuated = mixed[:, :ACT].reshape(STEPS * ACT, -1)
    sensed = mixed[:, ACT:].reshape(STEPS * SENS, -1)
    partial_gram = lax.dot_general(
        sensed, actuated, (((1,), (1,)), ((), ())), preferred_element_type=jnp.float32
    )
    scale = 4.0 / math.sqrt(planes * count * span * depth)
    gram = butterfly(partial_gram, ("batch", "space")) * scale
    return (state, gram)


def solution(mesh):
    in_specs = (
        P("batch", "space", None),
        P("batch", "space"),
        P("batch", "space", None),
        P("space", None, None),
        P("space", None, None),
    )
    out_specs = (P("batch", "space", None, None), P())
    return jax.shard_map(body, mesh=mesh, in_specs=in_specs, out_specs=out_specs, check_vma=False)
```

```python
import math

import jax
import jax.numpy as jnp
from jax import lax
from jax.sharding import PartitionSpec as P

STEPS = 2
ACT = 4
SENS = 4


def padded(value, axis, width, dim):
    peers, length = lax.axis_size(axis), value.shape[dim]
    up = [(i, (i + 1) % peers) for i in range(peers)]
    down = [(j, i) for i, j in up]
    last = lax.slice_in_dim(value, length - width, length, axis=dim)
    initial = lax.slice_in_dim(value, 0, width, axis=dim)
    before = lax.ppermute(last, axis, up)
    after = lax.ppermute(initial, axis, down)
    return jnp.concatenate([before, value, after], axis=dim)


def padded_shared(value, width, dim):
    peers, pair = lax.axis_size("space"), lax.axis_size("batch")
    if pair % 2:
        return padded(value, "space", width, dim)
    length = value.shape[dim]
    odd = lax.axis_index("batch") % 2 == 1
    last = lax.slice_in_dim(value, length - width, length, axis=dim)
    initial = lax.slice_in_dim(value, 0, width, axis=dim)
    routes = []
    for s in range(peers):
        for b in range(pair):
            ahead = (s + 1) % peers if b % 2 == 0 else (s - 1) % peers
            routes.append((s * pair + b, ahead * pair + b))
    got = lax.ppermute(jnp.where(odd, initial, last), ("space", "batch"), routes)
    other = lax.ppermute(got, "batch", [(b, b ^ 1) for b in range(pair)])
    before = jnp.where(odd, other, got)
    after = jnp.where(odd, got, other)
    return jnp.concatenate([before, value, after], axis=dim)


def pieces(x):
    out, rest = [], x
    for _ in range(3):
        part = lax.reduce_precision(rest, exponent_bits=8, mantissa_bits=7)
        out.append(part.astype(jnp.bfloat16))
        rest = rest - part
    return out


def select(onehot, values):
    total = None
    for part in pieces(values):
        term = jnp.einsum("fmk,fkd->fmd", onehot, part, preferred_element_type=jnp.float32)
        total = term if total is None else total + term
    return total


def prepare(coef, adjoint):
    diff_c = coef[0]
    vel_c = coef[1]
    pre_lap = jnp.where(adjoint, diff_c, 1.0)
    post_lap = jnp.where(adjoint, 1.0, diff_c)
    pre_dx = jnp.where(adjoint, vel_c, 1.0)
    post_dx = jnp.where(adjoint, 1.0, -vel_c)
    return (pre_lap, post_lap, pre_dx, post_dx)


def advance(extended, weights):
    pre_lap, post_lap, pre_dx, post_dx = weights
    lifted = pre_lap * extended
    moved = pre_dx * extended
    middle = lifted[:, 1:-1]
    padded_z = jnp.pad(middle, ((0, 0), (0, 0), (0, 0), (1, 1)))
    total = lifted[:, 2:] + lifted[:, :-2]
    total = total + jnp.roll(middle, -1, 2) + jnp.roll(middle, 1, 2)
    total = total + padded_z[..., 2:] + padded_z[..., :-2]
    lapl = total - 6.0 * middle
    slope = 0.5 * (moved[:, 2:] - moved[:, :-2])
    return extended[:, 1:-1] + post_lap[1:-1] * lapl + post_dx[1:-1] * slope


def butterfly(value, axes):
    for axis in axes:
        n = lax.axis_size(axis)
        step = 1
        while step < n:
            value = value + lax.ppermute(value, axis, [(i, i ^ step) for i in range(n)])
            step *= 2
    return value


def body(owner, offset, profile, diffusion, velocity):
    count = lax.axis_size("space")
    fields_dev, rows_dev = offset.shape
    planes, span, depth = diffusion.shape
    cap = 4 * rows_dev // count
    slots = count * cap
    col_rows = -(-cap // depth)

    target = owner[..., 0]
    earlier = jnp.tril(jnp.ones((rows_dev, rows_dev), jnp.bool_), -1)
    same = target[:, :, None] == target[:, None, :]
    rank = jnp.sum(jnp.logical_and(same, earlier[None]), axis=2)
    slot = target * cap + rank
    hit = slot[:, None, :] == lax.broadcasted_iota(jnp.int32, (fields_dev, slots, rows_dev), 1)
    send_vals = select(hit.astype(jnp.bfloat16), profile)
    send_cols = jnp.sum(jnp.where(hit, offset[:, None, :], 0), axis=2).astype(jnp.float32)
    send_cols = jnp.pad(send_cols.reshape(fields_dev, count, cap), ((0, 0), (0, 0), (0, col_rows * depth - cap)))
    payload = jnp.concatenate(
        [send_vals.reshape(fields_dev, count, cap, depth), send_cols.reshape(fields_dev, count, col_rows, depth)],
        axis=2,
    )
    got = lax.all_to_all(payload, "space", split_axis=1, concat_axis=1, tiled=True)
    got_vals = got[:, :, :cap].reshape(fields_dev, slots, depth)
    got_cols = got[:, :, cap:].reshape(fields_dev, count, col_rows * depth)[:, :, :cap]
    got_cols = got_cols.reshape(fields_dev, slots).astype(jnp.int32)

    place = got_cols[:, None, :] == lax.broadcasted_iota(jnp.int32, (fields_dev, planes * span, slots), 1)
    state = select(place.astype(jnp.bfloat16), got_vals).reshape(fields_dev, planes, span, depth)

    adjoint = lax.axis_index("batch") >= lax.axis_size("batch") // 2
    coef = jnp.stack([diffusion, velocity])
    rim = padded_shared(coef, STEPS, 1)
    weights = prepare(rim, adjoint)
    extended = padded(state, "space", STEPS, 1)

    pieces_ = []

    def record(current):
        snap = current.astype(jnp.bfloat16).reshape(fields_dev, -1)
        pieces_.append(lax.all_to_all(snap, "batch", split_axis=1, concat_axis=0, tiled=True))

    for step in range(STEPS):
        extended = advance(extended, weights)
        weights = tuple(w[1:-1] for w in weights)
        width = STEPS - 1 - step
        record(extended[:, width:extended.shape[1] - width])
    state = extended
    mixed = jnp.stack(pieces_)
    actuated = mixed[:, :ACT].reshape(STEPS * ACT, -1)
    sensed = mixed[:, ACT:].reshape(STEPS * SENS, -1)
    partial_gram = lax.dot_general(
        sensed, actuated, (((1,), (1,)), ((), ())), preferred_element_type=jnp.float32
    )
    scale = 4.0 / math.sqrt(planes * count * span * depth)
    gram = butterfly(partial_gram, ("batch", "space")) * scale
    return (state, gram)


def solution(mesh):
    in_specs = (
        P("batch", "space", None),
        P("batch", "space"),
        P("batch", "space", None),
        P("space", None, None),
        P("space", None, None),
    )
    out_specs = (P("batch", "space", None, None), P())
    return jax.shard_map(body, mesh=mesh, in_specs=in_specs, out_specs=out_specs, check_vma=False)
```

```python
import math

import jax
import jax.numpy as jnp
from jax import lax
from jax.sharding import PartitionSpec as P

STEPS = 2
ACT = 4
SENS = 4


LINK = jnp.bfloat16


def padded(value, axis, width, dim):
    peers, length = lax.axis_size(axis), value.shape[dim]
    up = [(i, (i + 1) % peers) for i in range(peers)]
    down = [(j, i) for i, j in up]
    last = lax.slice_in_dim(value, length - width, length, axis=dim).astype(LINK)
    initial = lax.slice_in_dim(value, 0, width, axis=dim).astype(LINK)
    before = lax.ppermute(last, axis, up).astype(value.dtype)
    after = lax.ppermute(initial, axis, down).astype(value.dtype)
    return jnp.concatenate([before, value, after], axis=dim)


def padded_shared(value, width, dim):
    peers, pair = lax.axis_size("space"), lax.axis_size("batch")
    if pair % 2:
        return padded(value, "space", width, dim)
    length = value.shape[dim]
    odd = lax.axis_index("batch") % 2 == 1
    last = lax.slice_in_dim(value, length - width, length, axis=dim)
    initial = lax.slice_in_dim(value, 0, width, axis=dim)
    routes = []
    for s in range(peers):
        for b in range(pair):
            ahead = (s + 1) % peers if b % 2 == 0 else (s - 1) % peers
            routes.append((s * pair + b, ahead * pair + b))
    got = lax.ppermute(jnp.where(odd, initial, last).astype(LINK), ("space", "batch"), routes)
    other = lax.ppermute(got, "batch", [(b, b ^ 1) for b in range(pair)]).astype(value.dtype)
    got = got.astype(value.dtype)
    before = jnp.where(odd, other, got)
    after = jnp.where(odd, got, other)
    return jnp.concatenate([before, value, after], axis=dim)


def pieces(x):
    out, rest = [], x
    for _ in range(3):
        part = lax.reduce_precision(rest, exponent_bits=8, mantissa_bits=7)
        out.append(part.astype(jnp.bfloat16))
        rest = rest - part
    return out


def select(onehot, values):
    total = None
    for part in pieces(values):
        term = jnp.einsum("fmk,fkd->fmd", onehot, part, preferred_element_type=jnp.float32)
        total = term if total is None else total + term
    return total


def prepare(coef, adjoint):
    diff_c = coef[0]
    vel_c = coef[1]
    pre_lap = jnp.where(adjoint, diff_c, 1.0)
    post_lap = jnp.where(adjoint, 1.0, diff_c)
    pre_dx = jnp.where(adjoint, vel_c, 1.0)
    post_dx = jnp.where(adjoint, 1.0, -vel_c)
    return (pre_lap, post_lap, pre_dx, post_dx)


def advance(extended, weights):
    pre_lap, post_lap, pre_dx, post_dx = weights
    lifted = pre_lap * extended
    moved = pre_dx * extended
    middle = lifted[:, 1:-1]
    padded_z = jnp.pad(middle, ((0, 0), (0, 0), (0, 0), (1, 1)))
    total = lifted[:, 2:] + lifted[:, :-2]
    total = total + jnp.roll(middle, -1, 2) + jnp.roll(middle, 1, 2)
    total = total + padded_z[..., 2:] + padded_z[..., :-2]
    lapl = total - 6.0 * middle
    slope = 0.5 * (moved[:, 2:] - moved[:, :-2])
    return extended[:, 1:-1] + post_lap[1:-1] * lapl + post_dx[1:-1] * slope


def butterfly(value, axes):
    for axis in axes:
        n = lax.axis_size(axis)
        step = 1
        while step < n:
            value = value + lax.ppermute(value, axis, [(i, i ^ step) for i in range(n)])
            step *= 2
    return value


def body(owner, offset, profile, diffusion, velocity):
    count = lax.axis_size("space")
    fields_dev, rows_dev = offset.shape
    planes, span, depth = diffusion.shape
    cap = 4 * rows_dev // count
    slots = count * cap
    col_rows = -(-cap // depth)

    target = owner[..., 0]
    earlier = jnp.tril(jnp.ones((rows_dev, rows_dev), jnp.bool_), -1)
    same = target[:, :, None] == target[:, None, :]
    rank = jnp.sum(jnp.logical_and(same, earlier[None]), axis=2)
    slot = target * cap + rank
    hit = slot[:, None, :] == lax.broadcasted_iota(jnp.int32, (fields_dev, slots, rows_dev), 1)
    send_vals = select(hit.astype(jnp.bfloat16), profile)
    send_cols = jnp.sum(jnp.where(hit, offset[:, None, :], 0), axis=2).astype(jnp.float32)
    send_cols = jnp.pad(send_cols.reshape(fields_dev, count, cap), ((0, 0), (0, 0), (0, col_rows * depth - cap)))
    payload = jnp.concatenate(
        [send_vals.reshape(fields_dev, count, cap, depth), send_cols.reshape(fields_dev, count, col_rows, depth)],
        axis=2,
    )
    got = lax.all_to_all(payload, "space", split_axis=1, concat_axis=1, tiled=True)
    got_vals = got[:, :, :cap].reshape(fields_dev, slots, depth)
    got_cols = got[:, :, cap:].reshape(fields_dev, count, col_rows * depth)[:, :, :cap]
    got_cols = got_cols.reshape(fields_dev, slots).astype(jnp.int32)

    place = got_cols[:, None, :] == lax.broadcasted_iota(jnp.int32, (fields_dev, planes * span, slots), 1)
    state = select(place.astype(jnp.bfloat16), got_vals).reshape(fields_dev, planes, span, depth)

    adjoint = lax.axis_index("batch") >= lax.axis_size("batch") // 2
    coef = jnp.stack([diffusion, velocity])
    rim = padded_shared(coef, STEPS, 1)
    weights = prepare(rim, adjoint)
    extended = padded(state, "space", STEPS, 1)

    pieces_ = []

    def record(current):
        snap = current.astype(jnp.bfloat16).reshape(fields_dev, -1)
        pieces_.append(lax.all_to_all(snap, "batch", split_axis=1, concat_axis=0, tiled=True))

    for step in range(STEPS):
        extended = advance(extended, weights)
        weights = tuple(w[1:-1] for w in weights)
        width = STEPS - 1 - step
        record(extended[:, width:extended.shape[1] - width])
    state = extended
    mixed = jnp.stack(pieces_)
    actuated = mixed[:, :ACT].reshape(STEPS * ACT, -1)
    sensed = mixed[:, ACT:].reshape(STEPS * SENS, -1)
    partial_gram = lax.dot_general(
        sensed, actuated, (((1,), (1,)), ((), ())), preferred_element_type=jnp.float32
    )
    scale = 4.0 / math.sqrt(planes * count * span * depth)
    gram = butterfly(partial_gram, ("batch", "space")) * scale
    return (state, gram)


def solution(mesh):
    in_specs = (
        P("batch", "space", None),
        P("batch", "space"),
        P("batch", "space", None),
        P("space", None, None),
        P("space", None, None),
    )
    out_specs = (P("batch", "space", None, None), P())
    return jax.shard_map(body, mesh=mesh, in_specs=in_specs, out_specs=out_specs, check_vma=False)
```

```python
import math

import jax
import jax.numpy as jnp
from jax import lax
from jax.sharding import PartitionSpec as P

STEPS = 2
ACT = 4
SENS = 4


LINK = jnp.bfloat16


def padded(value, axis, width, dim):
    peers, length = lax.axis_size(axis), value.shape[dim]
    up = [(i, (i + 1) % peers) for i in range(peers)]
    down = [(j, i) for i, j in up]
    last = lax.slice_in_dim(value, length - width, length, axis=dim).astype(LINK)
    initial = lax.slice_in_dim(value, 0, width, axis=dim).astype(LINK)
    before = lax.ppermute(last, axis, up).astype(value.dtype)
    after = lax.ppermute(initial, axis, down).astype(value.dtype)
    return jnp.concatenate([before, value, after], axis=dim)


def padded_shared(value, width, dim):
    peers, pair = lax.axis_size("space"), lax.axis_size("batch")
    if pair % 2:
        return padded(value, "space", width, dim)
    length = value.shape[dim]
    odd = lax.axis_index("batch") % 2 == 1
    last = lax.slice_in_dim(value, length - width, length, axis=dim)
    initial = lax.slice_in_dim(value, 0, width, axis=dim)
    routes = []
    for s in range(peers):
        for b in range(pair):
            ahead = (s + 1) % peers if b % 2 == 0 else (s - 1) % peers
            routes.append((s * pair + b, ahead * pair + b))
    got = lax.ppermute(jnp.where(odd, initial, last).astype(LINK), ("space", "batch"), routes)
    other = lax.ppermute(got, "batch", [(b, b ^ 1) for b in range(pair)]).astype(value.dtype)
    got = got.astype(value.dtype)
    before = jnp.where(odd, other, got)
    after = jnp.where(odd, got, other)
    return jnp.concatenate([before, value, after], axis=dim)


def pieces(x):
    out, rest = [], x
    for _ in range(3):
        part = lax.reduce_precision(rest, exponent_bits=8, mantissa_bits=7)
        out.append(part.astype(jnp.bfloat16))
        rest = rest - part
    return out


def select(onehot, values):
    depth = values.shape[-1]
    parts = pieces(values)
    terms = jnp.einsum("fmk,fkd->fmd", onehot, jnp.concatenate(parts, axis=-1), preferred_element_type=jnp.float32)
    total = terms[..., :depth]
    for i in range(1, len(parts)):
        total = total + terms[..., i * depth:(i + 1) * depth]
    return total


def prepare(coef, adjoint):
    diff_c = coef[0]
    vel_c = coef[1]
    pre_lap = jnp.where(adjoint, diff_c, 1.0)
    post_lap = jnp.where(adjoint, 1.0, diff_c)
    pre_dx = jnp.where(adjoint, vel_c, 1.0)
    post_dx = jnp.where(adjoint, 1.0, -vel_c)
    return (pre_lap, post_lap, pre_dx, post_dx)


def advance(extended, weights):
    pre_lap, post_lap, pre_dx, post_dx = weights
    lifted = pre_lap * extended
    moved = pre_dx * extended
    middle = lifted[:, 1:-1]
    padded_z = jnp.pad(middle, ((0, 0), (0, 0), (0, 0), (1, 1)))
    total = lifted[:, 2:] + lifted[:, :-2]
    total = total + jnp.roll(middle, -1, 2) + jnp.roll(middle, 1, 2)
    total = total + padded_z[..., 2:] + padded_z[..., :-2]
    lapl = total - 6.0 * middle
    slope = 0.5 * (moved[:, 2:] - moved[:, :-2])
    return extended[:, 1:-1] + post_lap[1:-1] * lapl + post_dx[1:-1] * slope


def butterfly(value, axes):
    for axis in axes:
        n = lax.axis_size(axis)
        step = 1
        while step < n:
            value = value + lax.ppermute(value, axis, [(i, i ^ step) for i in range(n)])
            step *= 2
    return value


def body(owner, offset, profile, diffusion, velocity):
    count = lax.axis_size("space")
    fields_dev, rows_dev = offset.shape
    planes, span, depth = diffusion.shape
    cap = 4 * rows_dev // count
    slots = count * cap
    col_rows = -(-cap // depth)

    target = owner[..., 0]
    earlier = jnp.tril(jnp.ones((rows_dev, rows_dev), jnp.bool_), -1)
    same = target[:, :, None] == target[:, None, :]
    rank = jnp.sum(jnp.logical_and(same, earlier[None]), axis=2)
    slot = target * cap + rank
    hit = slot[:, None, :] == lax.broadcasted_iota(jnp.int32, (fields_dev, slots, rows_dev), 1)
    send_vals = select(hit.astype(jnp.bfloat16), profile)
    send_cols = jnp.sum(jnp.where(hit, offset[:, None, :], 0), axis=2).astype(jnp.float32)
    send_cols = jnp.pad(send_cols.reshape(fields_dev, count, cap), ((0, 0), (0, 0), (0, col_rows * depth - cap)))
    payload = jnp.concatenate(
        [send_vals.reshape(fields_dev, count, cap, depth), send_cols.reshape(fields_dev, count, col_rows, depth)],
        axis=2,
    )
    got = lax.all_to_all(payload, "space", split_axis=1, concat_axis=1, tiled=True)
    got_vals = got[:, :, :cap].reshape(fields_dev, slots, depth)
    got_cols = got[:, :, cap:].reshape(fields_dev, count, col_rows * depth)[:, :, :cap]
    got_cols = got_cols.reshape(fields_dev, slots).astype(jnp.int32)

    place = got_cols[:, None, :] == lax.broadcasted_iota(jnp.int32, (fields_dev, planes * span, slots), 1)
    state = select(place.astype(jnp.bfloat16), got_vals).reshape(fields_dev, planes, span, depth)

    adjoint = lax.axis_index("batch") >= lax.axis_size("batch") // 2
    coef = jnp.stack([diffusion, velocity])
    rim = padded_shared(coef, STEPS, 1)
    weights = prepare(rim, adjoint)
    extended = padded(state, "space", STEPS, 1)

    share = lax.axis_size("batch")
    cut = 1 if planes % share == 0 else 2
    snaps = []
    for step in range(STEPS):
        extended = advance(extended, weights)
        weights = tuple(w[1:-1] for w in weights)
        width = STEPS - 1 - step
        snap = extended[:, width:extended.shape[1] - width].astype(jnp.bfloat16)
        mixed = lax.all_to_all(snap, "batch", split_axis=cut, concat_axis=0, tiled=True)
        snaps.append(mixed.reshape(mixed.shape[0], -1))
    state = extended
    rows = []
    for sensed in snaps:
        row = []
        for actuated in snaps:
            row.append(lax.dot_general(
                sensed[ACT:ACT + SENS], actuated[:ACT], (((1,), (1,)), ((), ())), preferred_element_type=jnp.float32
            ))
        rows.append(jnp.concatenate(row, axis=1))
    partial_gram = jnp.concatenate(rows, axis=0)
    scale = 4.0 / math.sqrt(planes * count * span * depth)
    gram = butterfly(partial_gram, ("batch", "space")) * scale
    return (state, gram)


def solution(mesh):
    in_specs = (
        P("batch", "space", None),
        P("batch", "space"),
        P("batch", "space", None),
        P("space", None, None),
        P("space", None, None),
    )
    out_specs = (P("batch", "space", None, None), P())
    return jax.shard_map(body, mesh=mesh, in_specs=in_specs, out_specs=out_specs, check_vma=False)
```

```python
import math

import jax
import jax.numpy as jnp
from jax import lax
from jax.experimental import pallas as pl
from jax.experimental.pallas import tpu as pltpu
from jax.sharding import PartitionSpec as P

STEPS = 2
ACT = 4
SENS = 4


LINK = jnp.bfloat16


def halos(value, axis, width, dim):
    peers, length = lax.axis_size(axis), value.shape[dim]
    up = [(i, (i + 1) % peers) for i in range(peers)]
    down = [(j, i) for i, j in up]
    last = lax.slice_in_dim(value, length - width, length, axis=dim).astype(LINK)
    initial = lax.slice_in_dim(value, 0, width, axis=dim).astype(LINK)
    return lax.ppermute(last, axis, up), lax.ppermute(initial, axis, down)


def halos_shared(value, width, dim):
    peers, pair = lax.axis_size("space"), lax.axis_size("batch")
    if pair % 2:
        return halos(value, "space", width, dim)
    length = value.shape[dim]
    odd = lax.axis_index("batch") % 2 == 1
    last = lax.slice_in_dim(value, length - width, length, axis=dim)
    initial = lax.slice_in_dim(value, 0, width, axis=dim)
    routes = []
    for s in range(peers):
        for b in range(pair):
            ahead = (s + 1) % peers if b % 2 == 0 else (s - 1) % peers
            routes.append((s * pair + b, ahead * pair + b))
    got = lax.ppermute(jnp.where(odd, initial, last).astype(LINK), ("space", "batch"), routes)
    other = lax.ppermute(got, "batch", [(b, b ^ 1) for b in range(pair)])
    return jnp.where(odd, other, got), jnp.where(odd, got, other)


ROWS = 8


def stencil_kernel(flag_ref, x_ref, xb_ref, xa_ref, d_ref, v_ref, cb_ref, ca_ref, out_ref, s1_ref, s2_ref, mid_ref):
    planes, span, depth = x_ref.shape[1], x_ref.shape[2], x_ref.shape[3]
    halo = xb_ref.shape[1]
    ext = planes + 2 * halo
    tiles = span // ROWS
    sub = lax.broadcasted_iota(jnp.int32, (ROWS, depth), 0)
    lane = lax.broadcasted_iota(jnp.int32, (ROWS, depth), 1)

    def rows(c):
        return pl.ds(pl.multiple_of(c * ROWS, ROWS), ROWS)

    def level0(k, c):
        if k < halo:
            return xb_ref[0, k, rows(c), :].astype(jnp.float32)
        if k < halo + planes:
            return x_ref[0, k - halo, rows(c), :]
        return xa_ref[0, k - halo - planes, rows(c), :].astype(jnp.float32)

    def level1(k, c):
        return mid_ref[k - 1, rows(c), :]

    def coef(which, k, c):
        if k < halo:
            return cb_ref[which, k, rows(c), :].astype(jnp.float32)
        if k < halo + planes:
            return (d_ref if which == 0 else v_ref)[k - halo, rows(c), :]
        return ca_ref[which, k - halo - planes, rows(c), :].astype(jnp.float32)

    def lap(m, zero, p, before, after):
        total = p + m
        up = jnp.where(sub == ROWS - 1, pltpu.roll(after, ROWS - 1, 0), pltpu.roll(zero, ROWS - 1, 0))
        down = jnp.where(sub == 0, pltpu.roll(before, 1, 0), pltpu.roll(zero, 1, 0))
        total = total + up + down
        zu = jnp.where(lane == depth - 1, 0.0, pltpu.roll(zero, depth - 1, 1))
        zd = jnp.where(lane == 0, 0.0, pltpu.roll(zero, 1, 1))
        total = total + zu + zd
        return total - 6.0 * zero

    def update(load, k, c, adjoint):
        prev, nxt = (c + tiles - 1) % tiles, (c + 1) % tiles
        xm, x0, xp = load(k - 1, c), load(k, c), load(k + 1, c)
        xbefore, xafter = load(k, prev), load(k, nxt)
        if adjoint:
            lifted = lap(coef(0, k - 1, c) * xm, coef(0, k, c) * x0, coef(0, k + 1, c) * xp,
                         coef(0, k, prev) * xbefore, coef(0, k, nxt) * xafter)
            slope = 0.5 * (coef(1, k + 1, c) * xp - coef(1, k - 1, c) * xm)
            return x0 + lifted + slope
        lifted = lap(xm, x0, xp, xbefore, xafter)
        slope = 0.5 * (xp - xm)
        return x0 + coef(0, k, c) * lifted - coef(1, k, c) * slope

    def run(adjoint):
        for k in range(1, ext - 1):
            def first(c, carry, k=k):
                value = update(level0, k, c, adjoint)
                mid_ref[k - 1, rows(c), :] = value
                if halo <= k < halo + planes:
                    s1_ref[0, k - halo, rows(c), :] = value.astype(s1_ref.dtype)
                return carry
            lax.fori_loop(0, tiles, first, 0, unroll=2)
        for k in range(halo, halo + planes):
            def second(c, carry, k=k):
                value = update(level1, k, c, adjoint)
                out_ref[0, k - halo, rows(c), :] = value
                s2_ref[0, k - halo, rows(c), :] = value.astype(s2_ref.dtype)
                return carry
            lax.fori_loop(0, tiles, second, 0, unroll=2)

    @pl.when(flag_ref[0] == 0)
    def _():
        run(False)

    @pl.when(flag_ref[0] != 0)
    def _():
        run(True)


def two_steps(flag, state, before, after, diffusion, velocity, coef_before, coef_after):
    fields, planes, span, depth = state.shape
    halo = before.shape[1]
    field_block = lambda n: pl.BlockSpec((1, n, span, depth), lambda f: (f, 0, 0, 0))
    whole = lambda shape: pl.BlockSpec(shape, lambda f: (0,) * len(shape))
    return pl.pallas_call(
        stencil_kernel,
        grid=(fields,),
        in_specs=[
            pl.BlockSpec(memory_space=pltpu.SMEM),
            field_block(planes),
            field_block(halo),
            field_block(halo),
            whole((planes, span, depth)),
            whole((planes, span, depth)),
            whole((2, halo, span, depth)),
            whole((2, halo, span, depth)),
        ],
        out_specs=[field_block(planes), field_block(planes), field_block(planes)],
        out_shape=[
            jax.ShapeDtypeStruct(state.shape, jnp.float32),
            jax.ShapeDtypeStruct(state.shape, jnp.bfloat16),
            jax.ShapeDtypeStruct(state.shape, jnp.bfloat16),
        ],
        scratch_shapes=[pltpu.VMEM((planes + 2 * halo - 2, span, depth), jnp.float32)],
        compiler_params=pltpu.CompilerParams(dimension_semantics=("arbitrary",)),
    )(flag, state, before, after, diffusion, velocity, coef_before, coef_after)


def pieces(x):
    out, rest = [], x
    for _ in range(3):
        part = lax.reduce_precision(rest, exponent_bits=8, mantissa_bits=7)
        out.append(part.astype(jnp.bfloat16))
        rest = rest - part
    return out


def select(onehot, values):
    depth = values.shape[-1]
    parts = pieces(values)
    terms = jnp.einsum("fmk,fkd->fmd", onehot, jnp.concatenate(parts, axis=-1), preferred_element_type=jnp.float32)
    total = terms[..., :depth]
    for i in range(1, len(parts)):
        total = total + terms[..., i * depth:(i + 1) * depth]
    return total


def butterfly(value, axes):
    for axis in axes:
        n = lax.axis_size(axis)
        step = 1
        while step < n:
            value = value + lax.ppermute(value, axis, [(i, i ^ step) for i in range(n)])
            step *= 2
    return value


def body(owner, offset, profile, diffusion, velocity):
    count = lax.axis_size("space")
    fields_dev, rows_dev = offset.shape
    planes, span, depth = diffusion.shape
    cap = 4 * rows_dev // count
    slots = count * cap
    col_rows = -(-cap // depth)

    target = owner[..., 0]
    earlier = jnp.tril(jnp.ones((rows_dev, rows_dev), jnp.bool_), -1)
    same = target[:, :, None] == target[:, None, :]
    rank = jnp.sum(jnp.logical_and(same, earlier[None]), axis=2)
    slot = target * cap + rank
    hit = slot[:, None, :] == lax.broadcasted_iota(jnp.int32, (fields_dev, slots, rows_dev), 1)
    send_vals = select(hit.astype(jnp.bfloat16), profile)
    send_cols = jnp.sum(jnp.where(hit, offset[:, None, :], 0), axis=2).astype(jnp.float32)
    send_cols = jnp.pad(send_cols.reshape(fields_dev, count, cap), ((0, 0), (0, 0), (0, col_rows * depth - cap)))
    payload = jnp.concatenate(
        [send_vals.reshape(fields_dev, count, cap, depth), send_cols.reshape(fields_dev, count, col_rows, depth)],
        axis=2,
    )
    got = lax.all_to_all(payload, "space", split_axis=1, concat_axis=1, tiled=True)
    got_vals = got[:, :, :cap].reshape(fields_dev, slots, depth)
    got_cols = got[:, :, cap:].reshape(fields_dev, count, col_rows * depth)[:, :, :cap]
    got_cols = got_cols.reshape(fields_dev, slots).astype(jnp.int32)

    place = got_cols[:, None, :] == lax.broadcasted_iota(jnp.int32, (fields_dev, planes * span, slots), 1)
    state = select(place.astype(jnp.bfloat16), got_vals).reshape(fields_dev, planes, span, depth)

    adjoint = lax.axis_index("batch") >= lax.axis_size("batch") // 2
    flag = adjoint.astype(jnp.int32).reshape(1)
    coef_before, coef_after = halos_shared(jnp.stack([diffusion, velocity]), STEPS, 1)
    before, after = halos(state, "space", STEPS, 1)
    state, snap1, snap2 = two_steps(flag, state, before, after, diffusion, velocity, coef_before, coef_after)

    share = lax.axis_size("batch")
    cut = 1 if planes % share == 0 else 2
    snaps = []
    for snap in (snap1, snap2):
        mixed = lax.all_to_all(snap, "batch", split_axis=cut, concat_axis=0, tiled=True)
        snaps.append(mixed.reshape(mixed.shape[0], -1))
    rows = []
    for sensed in snaps:
        row = []
        for actuated in snaps:
            row.append(lax.dot_general(
                sensed[ACT:ACT + SENS], actuated[:ACT], (((1,), (1,)), ((), ())), preferred_element_type=jnp.float32
            ))
        rows.append(jnp.concatenate(row, axis=1))
    partial_gram = jnp.concatenate(rows, axis=0)
    scale = 4.0 / math.sqrt(planes * count * span * depth)
    gram = butterfly(partial_gram, ("batch", "space")) * scale
    return (state, gram)


def solution(mesh):
    in_specs = (
        P("batch", "space", None),
        P("batch", "space"),
        P("batch", "space", None),
        P("space", None, None),
        P("space", None, None),
    )
    out_specs = (P("batch", "space", None, None), P())
    return jax.shard_map(body, mesh=mesh, in_specs=in_specs, out_specs=out_specs, check_vma=False)
```

```python
import math

import jax
import jax.numpy as jnp
from jax import lax
from jax.experimental import pallas as pl
from jax.experimental.pallas import tpu as pltpu
from jax.sharding import PartitionSpec as P

STEPS = 2
ACT = 4
SENS = 4


LINK = jnp.bfloat16


def halos(value, axis, width, dim):
    peers, length = lax.axis_size(axis), value.shape[dim]
    up = [(i, (i + 1) % peers) for i in range(peers)]
    down = [(j, i) for i, j in up]
    last = lax.slice_in_dim(value, length - width, length, axis=dim).astype(LINK)
    initial = lax.slice_in_dim(value, 0, width, axis=dim).astype(LINK)
    return lax.ppermute(last, axis, up), lax.ppermute(initial, axis, down)


def halos_shared(value, width, dim):
    peers, pair = lax.axis_size("space"), lax.axis_size("batch")
    if pair % 2:
        return halos(value, "space", width, dim)
    length = value.shape[dim]
    odd = lax.axis_index("batch") % 2 == 1
    last = lax.slice_in_dim(value, length - width, length, axis=dim)
    initial = lax.slice_in_dim(value, 0, width, axis=dim)
    routes = []
    for s in range(peers):
        for b in range(pair):
            ahead = (s + 1) % peers if b % 2 == 0 else (s - 1) % peers
            routes.append((s * pair + b, ahead * pair + b))
    got = lax.ppermute(jnp.where(odd, initial, last).astype(LINK), ("space", "batch"), routes)
    other = lax.ppermute(got, "batch", [(b, b ^ 1) for b in range(pair)])
    return jnp.where(odd, other, got), jnp.where(odd, got, other)


ROWS = 256


def stencil_kernel(flag_ref, x_ref, xb_ref, xa_ref, d_ref, v_ref, cb_ref, ca_ref, out_ref, s1_ref, s2_ref, mid_ref):
    planes, span, depth = x_ref.shape[1], x_ref.shape[2], x_ref.shape[3]
    halo = xb_ref.shape[1]
    ext = planes + 2 * halo
    block = math.gcd(span, ROWS)
    tiles = span // block
    sub = lax.broadcasted_iota(jnp.int32, (block, depth), 0)
    lane = lax.broadcasted_iota(jnp.int32, (block, depth), 1)

    def rows(c):
        return pl.ds(pl.multiple_of(c * block, block), block)

    def level0(k, c):
        if k < halo:
            return xb_ref[0, k, rows(c), :].astype(jnp.float32)
        if k < halo + planes:
            return x_ref[0, k - halo, rows(c), :]
        return xa_ref[0, k - halo - planes, rows(c), :].astype(jnp.float32)

    def level1(k, c):
        return mid_ref[k - 1, rows(c), :]

    def coef(which, k, c):
        if k < halo:
            return cb_ref[which, k, rows(c), :].astype(jnp.float32)
        if k < halo + planes:
            return (d_ref if which == 0 else v_ref)[k - halo, rows(c), :]
        return ca_ref[which, k - halo - planes, rows(c), :].astype(jnp.float32)

    def lap(m, zero, p, before, after):
        total = p + m
        up = jnp.where(sub == block - 1, pltpu.roll(after, block - 1, 0), pltpu.roll(zero, block - 1, 0))
        down = jnp.where(sub == 0, pltpu.roll(before, 1, 0), pltpu.roll(zero, 1, 0))
        total = total + up + down
        zu = jnp.where(lane == depth - 1, 0.0, pltpu.roll(zero, depth - 1, 1))
        zd = jnp.where(lane == 0, 0.0, pltpu.roll(zero, 1, 1))
        total = total + zu + zd
        return total - 6.0 * zero

    def update(load, k, c, adjoint):
        prev, nxt = (c + tiles - 1) % tiles, (c + 1) % tiles
        xm, x0, xp = load(k - 1, c), load(k, c), load(k + 1, c)
        xbefore, xafter = load(k, prev), load(k, nxt)
        if adjoint:
            lifted = lap(coef(0, k - 1, c) * xm, coef(0, k, c) * x0, coef(0, k + 1, c) * xp,
                         coef(0, k, prev) * xbefore, coef(0, k, nxt) * xafter)
            slope = 0.5 * (coef(1, k + 1, c) * xp - coef(1, k - 1, c) * xm)
            return x0 + lifted + slope
        lifted = lap(xm, x0, xp, xbefore, xafter)
        slope = 0.5 * (xp - xm)
        return x0 + coef(0, k, c) * lifted - coef(1, k, c) * slope

    def run(adjoint):
        for k in range(1, ext - 1):
            def first(c, carry, k=k):
                value = update(level0, k, c, adjoint)
                mid_ref[k - 1, rows(c), :] = value
                if halo <= k < halo + planes:
                    s1_ref[0, k - halo, rows(c), :] = value.astype(s1_ref.dtype)
                return carry
            lax.fori_loop(0, tiles, first, 0, unroll=2)
        for k in range(halo, halo + planes):
            def second(c, carry, k=k):
                value = update(level1, k, c, adjoint)
                out_ref[0, k - halo, rows(c), :] = value
                s2_ref[0, k - halo, rows(c), :] = value.astype(s2_ref.dtype)
                return carry
            lax.fori_loop(0, tiles, second, 0, unroll=2)

    @pl.when(flag_ref[0] == 0)
    def _():
        run(False)

    @pl.when(flag_ref[0] != 0)
    def _():
        run(True)


def two_steps(flag, state, before, after, diffusion, velocity, coef_before, coef_after):
    fields, planes, span, depth = state.shape
    halo = before.shape[1]
    field_block = lambda n: pl.BlockSpec((1, n, span, depth), lambda f: (f, 0, 0, 0))
    whole = lambda shape: pl.BlockSpec(shape, lambda f: (0,) * len(shape))
    return pl.pallas_call(
        stencil_kernel,
        grid=(fields,),
        in_specs=[
            pl.BlockSpec(memory_space=pltpu.SMEM),
            field_block(planes),
            field_block(halo),
            field_block(halo),
            whole((planes, span, depth)),
            whole((planes, span, depth)),
            whole((2, halo, span, depth)),
            whole((2, halo, span, depth)),
        ],
        out_specs=[field_block(planes), field_block(planes), field_block(planes)],
        out_shape=[
            jax.ShapeDtypeStruct(state.shape, jnp.float32),
            jax.ShapeDtypeStruct(state.shape, jnp.bfloat16),
            jax.ShapeDtypeStruct(state.shape, jnp.bfloat16),
        ],
        scratch_shapes=[pltpu.VMEM((planes + 2 * halo - 2, span, depth), jnp.float32)],
        compiler_params=pltpu.CompilerParams(dimension_semantics=("arbitrary",)),
    )(flag, state, before, after, diffusion, velocity, coef_before, coef_after)


def pieces(x):
    out, rest = [], x
    for _ in range(3):
        part = lax.reduce_precision(rest, exponent_bits=8, mantissa_bits=7)
        out.append(part.astype(jnp.bfloat16))
        rest = rest - part
    return out


def select(onehot, values):
    depth = values.shape[-1]
    parts = pieces(values)
    terms = jnp.einsum("fmk,fkd->fmd", onehot, jnp.concatenate(parts, axis=-1), preferred_element_type=jnp.float32)
    total = terms[..., :depth]
    for i in range(1, len(parts)):
        total = total + terms[..., i * depth:(i + 1) * depth]
    return total


def butterfly(value, axes):
    for axis in axes:
        n = lax.axis_size(axis)
        step = 1
        while step < n:
            value = value + lax.ppermute(value, axis, [(i, i ^ step) for i in range(n)])
            step *= 2
    return value


def body(owner, offset, profile, diffusion, velocity):
    count = lax.axis_size("space")
    fields_dev, rows_dev = offset.shape
    planes, span, depth = diffusion.shape
    cap = 4 * rows_dev // count
    slots = count * cap
    col_rows = -(-cap // depth)

    target = owner[..., 0]
    earlier = jnp.tril(jnp.ones((rows_dev, rows_dev), jnp.bool_), -1)
    same = target[:, :, None] == target[:, None, :]
    rank = jnp.sum(jnp.logical_and(same, earlier[None]), axis=2)
    slot = target * cap + rank
    hit = slot[:, None, :] == lax.broadcasted_iota(jnp.int32, (fields_dev, slots, rows_dev), 1)
    send_vals = select(hit.astype(jnp.bfloat16), profile)
    send_cols = jnp.sum(jnp.where(hit, offset[:, None, :], 0), axis=2).astype(jnp.float32)
    send_cols = jnp.pad(send_cols.reshape(fields_dev, count, cap), ((0, 0), (0, 0), (0, col_rows * depth - cap)))
    payload = jnp.concatenate(
        [send_vals.reshape(fields_dev, count, cap, depth), send_cols.reshape(fields_dev, count, col_rows, depth)],
        axis=2,
    )
    got = lax.all_to_all(payload, "space", split_axis=1, concat_axis=1, tiled=True)
    got_vals = got[:, :, :cap].reshape(fields_dev, slots, depth)
    got_cols = got[:, :, cap:].reshape(fields_dev, count, col_rows * depth)[:, :, :cap]
    got_cols = got_cols.reshape(fields_dev, slots).astype(jnp.int32)

    place = got_cols[:, None, :] == lax.broadcasted_iota(jnp.int32, (fields_dev, planes * span, slots), 1)
    state = select(place.astype(jnp.bfloat16), got_vals).reshape(fields_dev, planes, span, depth)

    adjoint = lax.axis_index("batch") >= lax.axis_size("batch") // 2
    flag = adjoint.astype(jnp.int32).reshape(1)
    coef_before, coef_after = halos_shared(jnp.stack([diffusion, velocity]), STEPS, 1)
    before, after = halos(state, "space", STEPS, 1)
    state, snap1, snap2 = two_steps(flag, state, before, after, diffusion, velocity, coef_before, coef_after)

    share = lax.axis_size("batch")
    cut = 1 if planes % share == 0 else 2
    snaps = []
    for snap in (snap1, snap2):
        mixed = lax.all_to_all(snap, "batch", split_axis=cut, concat_axis=0, tiled=True)
        snaps.append(mixed.reshape(mixed.shape[0], -1))
    rows = []
    for sensed in snaps:
        row = []
        for actuated in snaps:
            row.append(lax.dot_general(
                sensed[ACT:ACT + SENS], actuated[:ACT], (((1,), (1,)), ((), ())), preferred_element_type=jnp.float32
            ))
        rows.append(jnp.concatenate(row, axis=1))
    partial_gram = jnp.concatenate(rows, axis=0)
    scale = 4.0 / math.sqrt(planes * count * span * depth)
    gram = butterfly(partial_gram, ("batch", "space")) * scale
    return (state, gram)


def solution(mesh):
    in_specs = (
        P("batch", "space", None),
        P("batch", "space"),
        P("batch", "space", None),
        P("space", None, None),
        P("space", None, None),
    )
    out_specs = (P("batch", "space", None, None), P())
    return jax.shard_map(body, mesh=mesh, in_specs=in_specs, out_specs=out_specs, check_vma=False)
```

```python
import math

import jax
import jax.numpy as jnp
from jax import lax
from jax.experimental import pallas as pl
from jax.experimental.pallas import tpu as pltpu
from jax.sharding import PartitionSpec as P

STEPS = 2
ACT = 4
SENS = 4


LINK = jnp.bfloat16


def halos(value, axis, width, dim):
    peers, length = lax.axis_size(axis), value.shape[dim]
    up = [(i, (i + 1) % peers) for i in range(peers)]
    down = [(j, i) for i, j in up]
    last = lax.slice_in_dim(value, length - width, length, axis=dim).astype(LINK)
    initial = lax.slice_in_dim(value, 0, width, axis=dim).astype(LINK)
    return lax.ppermute(last, axis, up), lax.ppermute(initial, axis, down)


def halos_shared(value, width, dim):
    peers, pair = lax.axis_size("space"), lax.axis_size("batch")
    if pair % 2:
        return halos(value, "space", width, dim)
    length = value.shape[dim]
    odd = lax.axis_index("batch") % 2 == 1
    last = lax.slice_in_dim(value, length - width, length, axis=dim)
    initial = lax.slice_in_dim(value, 0, width, axis=dim)
    routes = []
    for s in range(peers):
        for b in range(pair):
            ahead = (s + 1) % peers if b % 2 == 0 else (s - 1) % peers
            routes.append((s * pair + b, ahead * pair + b))
    got = lax.ppermute(jnp.where(odd, initial, last).astype(LINK), ("space", "batch"), routes)
    other = lax.ppermute(got, "batch", [(b, b ^ 1) for b in range(pair)])
    return jnp.where(odd, other, got), jnp.where(odd, got, other)


ROWS = 256


def stencil_parts(flag_ref, x_ref, xb_ref, xa_ref, d_ref, v_ref, cb_ref, ca_ref, halo):
    planes, span, depth = x_ref.shape[1], x_ref.shape[2], x_ref.shape[3]
    block = math.gcd(span, ROWS)
    tiles = span // block
    sub = lax.broadcasted_iota(jnp.int32, (block, depth), 0)
    lane = lax.broadcasted_iota(jnp.int32, (block, depth), 1)

    def rows(c):
        return pl.ds(pl.multiple_of(c * block, block), block)

    def level0(k, c):
        if k < halo:
            return xb_ref[0, k, rows(c), :].astype(jnp.float32)
        if k < halo + planes:
            return x_ref[0, k - halo, rows(c), :]
        return xa_ref[0, k - halo - planes, rows(c), :].astype(jnp.float32)

    def coef(which, k, c):
        if k < halo:
            return cb_ref[which, k, rows(c), :].astype(jnp.float32)
        if k < halo + planes:
            return (d_ref if which == 0 else v_ref)[k - halo, rows(c), :]
        return ca_ref[which, k - halo - planes, rows(c), :].astype(jnp.float32)

    def lap(m, zero, p, before, after):
        total = p + m
        up = jnp.where(sub == block - 1, pltpu.roll(after, block - 1, 0), pltpu.roll(zero, block - 1, 0))
        down = jnp.where(sub == 0, pltpu.roll(before, 1, 0), pltpu.roll(zero, 1, 0))
        total = total + up + down
        zu = jnp.where(lane == depth - 1, 0.0, pltpu.roll(zero, depth - 1, 1))
        zd = jnp.where(lane == 0, 0.0, pltpu.roll(zero, 1, 1))
        total = total + zu + zd
        return total - 6.0 * zero

    def update(load, k, c, adjoint):
        prev, nxt = (c + tiles - 1) % tiles, (c + 1) % tiles
        xm, x0, xp = load(k - 1, c), load(k, c), load(k + 1, c)
        xbefore, xafter = load(k, prev), load(k, nxt)
        if adjoint:
            lifted = lap(coef(0, k - 1, c) * xm, coef(0, k, c) * x0, coef(0, k + 1, c) * xp,
                         coef(0, k, prev) * xbefore, coef(0, k, nxt) * xafter)
            slope = 0.5 * (coef(1, k + 1, c) * xp - coef(1, k - 1, c) * xm)
            return x0 + lifted + slope
        lifted = lap(xm, x0, xp, xbefore, xafter)
        slope = 0.5 * (xp - xm)
        return x0 + coef(0, k, c) * lifted - coef(1, k, c) * slope

    def both(run):
        @pl.when(flag_ref[0] == 0)
        def _():
            run(False)

        @pl.when(flag_ref[0] != 0)
        def _():
            run(True)

    return planes, tiles, rows, level0, update, both


def interior_kernel(flag_ref, x_ref, d_ref, v_ref, s_ref):
    halo = STEPS
    planes, tiles, rows, level0, update, both = stencil_parts(
        flag_ref, x_ref, None, None, d_ref, v_ref, None, None, halo)

    def run(adjoint):
        for k in range(halo + 1, halo + planes - 1):
            def first(c, carry, k=k):
                s_ref[0, k - halo - 1, rows(c), :] = update(level0, k, c, adjoint).astype(s_ref.dtype)
                return carry

            lax.fori_loop(0, tiles, first, 0, unroll=2)

    both(run)


def stencil_kernel(flag_ref, x_ref, xb_ref, xa_ref, d_ref, v_ref, cb_ref, ca_ref, out_ref, s1_ref, s2_ref, mid_ref):
    halo = xb_ref.shape[1]
    planes, tiles, rows, level0, update, both = stencil_parts(
        flag_ref, x_ref, xb_ref, xa_ref, d_ref, v_ref, cb_ref, ca_ref, halo)
    ext = planes + 2 * halo

    def level1(k, c):
        return mid_ref[k - 1, rows(c), :]

    def run(adjoint):
        for k in range(1, ext - 1):
            def first(c, carry, k=k):
                value = update(level0, k, c, adjoint)
                mid_ref[k - 1, rows(c), :] = value
                if k == halo or k == halo + planes - 1:
                    s1_ref[0, 0 if k == halo else 1, rows(c), :] = value.astype(s1_ref.dtype)
                return carry

            lax.fori_loop(0, tiles, first, 0, unroll=2)
        for k in range(halo, halo + planes):
            def second(c, carry, k=k):
                value = update(level1, k, c, adjoint)
                out_ref[0, k - halo, rows(c), :] = value
                s2_ref[0, k - halo, rows(c), :] = value.astype(s2_ref.dtype)
                return carry

            lax.fori_loop(0, tiles, second, 0, unroll=2)

    both(run)


def interior_step(flag, state, diffusion, velocity):
    fields, planes, span, depth = state.shape
    return pl.pallas_call(
        interior_kernel,
        grid=(fields,),
        in_specs=[
            pl.BlockSpec(memory_space=pltpu.SMEM),
            pl.BlockSpec((1, planes, span, depth), lambda f: (f, 0, 0, 0)),
            pl.BlockSpec((planes, span, depth), lambda f: (0, 0, 0)),
            pl.BlockSpec((planes, span, depth), lambda f: (0, 0, 0)),
        ],
        out_specs=pl.BlockSpec((1, planes - 2, span, depth), lambda f: (f, 0, 0, 0)),
        out_shape=jax.ShapeDtypeStruct((fields, planes - 2, span, depth), jnp.bfloat16),
        compiler_params=pltpu.CompilerParams(dimension_semantics=("arbitrary",)),
    )(flag, state, diffusion, velocity)


def two_steps(flag, state, before, after, diffusion, velocity, coef_before, coef_after):
    fields, planes, span, depth = state.shape
    halo = before.shape[1]
    field_block = lambda n: pl.BlockSpec((1, n, span, depth), lambda f: (f, 0, 0, 0))
    whole = lambda shape: pl.BlockSpec(shape, lambda f: (0,) * len(shape))
    return pl.pallas_call(
        stencil_kernel,
        grid=(fields,),
        in_specs=[
            pl.BlockSpec(memory_space=pltpu.SMEM),
            field_block(planes),
            field_block(halo),
            field_block(halo),
            whole((planes, span, depth)),
            whole((planes, span, depth)),
            whole((2, halo, span, depth)),
            whole((2, halo, span, depth)),
        ],
        out_specs=[field_block(planes), field_block(2), field_block(planes)],
        out_shape=[
            jax.ShapeDtypeStruct(state.shape, jnp.float32),
            jax.ShapeDtypeStruct((fields, 2, span, depth), jnp.bfloat16),
            jax.ShapeDtypeStruct(state.shape, jnp.bfloat16),
        ],
        scratch_shapes=[pltpu.VMEM((planes + 2 * halo - 2, span, depth), jnp.float32)],
        compiler_params=pltpu.CompilerParams(dimension_semantics=("arbitrary",)),
    )(flag, state, before, after, diffusion, velocity, coef_before, coef_after)


def pieces(x):
    out, rest = [], x
    for _ in range(3):
        part = lax.reduce_precision(rest, exponent_bits=8, mantissa_bits=7)
        out.append(part.astype(jnp.bfloat16))
        rest = rest - part
    return out


def select(onehot, values):
    depth = values.shape[-1]
    parts = pieces(values)
    terms = jnp.einsum("fmk,fkd->fmd", onehot, jnp.concatenate(parts, axis=-1), preferred_element_type=jnp.float32)
    total = terms[..., :depth]
    for i in range(1, len(parts)):
        total = total + terms[..., i * depth:(i + 1) * depth]
    return total


def butterfly(value, axes):
    for axis in axes:
        n = lax.axis_size(axis)
        step = 1
        while step < n:
            value = value + lax.ppermute(value, axis, [(i, i ^ step) for i in range(n)])
            step *= 2
    return value


def work(owner, offset, profile, diffusion, velocity):
    count = lax.axis_size("space")
    fields_dev, rows_dev = offset.shape
    planes, span, depth = diffusion.shape
    cap = 4 * rows_dev // count
    slots = count * cap
    col_rows = -(-cap // depth)

    target = owner[..., 0]
    earlier = jnp.tril(jnp.ones((rows_dev, rows_dev), jnp.bool_), -1)
    same = target[:, :, None] == target[:, None, :]
    rank = jnp.sum(jnp.logical_and(same, earlier[None]), axis=2)
    slot = target * cap + rank
    hit = slot[:, None, :] == lax.broadcasted_iota(jnp.int32, (fields_dev, slots, rows_dev), 1)
    send_vals = select(hit.astype(jnp.bfloat16), profile)
    send_cols = jnp.sum(jnp.where(hit, offset[:, None, :], 0), axis=2).astype(jnp.float32)
    send_cols = jnp.pad(send_cols.reshape(fields_dev, count, cap), ((0, 0), (0, 0), (0, col_rows * depth - cap)))
    payload = jnp.concatenate(
        [send_vals.reshape(fields_dev, count, cap, depth), send_cols.reshape(fields_dev, count, col_rows, depth)],
        axis=2,
    )
    got = lax.all_to_all(payload, "space", split_axis=1, concat_axis=1, tiled=True)
    got_vals = got[:, :, :cap].reshape(fields_dev, slots, depth)
    got_cols = got[:, :, cap:].reshape(fields_dev, count, col_rows * depth)[:, :, :cap]
    got_cols = got_cols.reshape(fields_dev, slots).astype(jnp.int32)

    place = got_cols[:, None, :] == lax.broadcasted_iota(jnp.int32, (fields_dev, planes * span, slots), 1)
    state = select(place.astype(jnp.bfloat16), got_vals).reshape(fields_dev, planes, span, depth)

    adjoint = lax.axis_index("batch") >= lax.axis_size("batch") // 2
    flag = adjoint.astype(jnp.int32).reshape(1)
    coef_before, coef_after = halos_shared(jnp.stack([diffusion, velocity]), STEPS, 1)
    inner = interior_step(flag, state, diffusion, velocity)
    before, after = halos(state, "space", STEPS, 1)
    state, outer, snap2 = two_steps(flag, state, before, after, diffusion, velocity, coef_before, coef_after)

    def spread(snap):
        return lax.all_to_all(snap, "batch", split_axis=2, concat_axis=0, tiled=True)

    inner, outer = spread(inner), spread(outer)
    first = jnp.concatenate([outer[:, :1], inner, outer[:, 1:]], axis=1)
    second = spread(snap2)
    snaps = [first.reshape(first.shape[0], -1), second.reshape(second.shape[0], -1)]
    rows = []
    for sensed in snaps:
        row = []
        for actuated in snaps:
            row.append(lax.dot_general(
                sensed[ACT:ACT + SENS], actuated[:ACT], (((1,), (1,)), ((), ())), preferred_element_type=jnp.float32
            ))
        rows.append(jnp.concatenate(row, axis=1))
    partial_gram = jnp.concatenate(rows, axis=0)
    scale = 4.0 / math.sqrt(planes * count * span * depth)
    gram = butterfly(partial_gram, ("batch", "space")) * scale
    return (state, gram)


def solution(mesh):
    in_specs = (
        P("batch", "space", None),
        P("batch", "space"),
        P("batch", "space", None),
        P("space", None, None),
        P("space", None, None),
    )
    out_specs = (P("batch", "space", None, None), P())
    return jax.shard_map(work, mesh=mesh, in_specs=in_specs, out_specs=out_specs, check_vma=False)
```

```python
import math

import jax
import jax.numpy as jnp
from jax import lax
from jax.experimental import pallas as pl
from jax.experimental.pallas import tpu as pltpu
from jax.sharding import PartitionSpec as P

STEPS = 2
ACT = 4
SENS = 4


LINK = jnp.bfloat16


def halos(value, axis, width, dim):
    peers, length = lax.axis_size(axis), value.shape[dim]
    up = [(i, (i + 1) % peers) for i in range(peers)]
    down = [(j, i) for i, j in up]
    last = lax.slice_in_dim(value, length - width, length, axis=dim).astype(LINK)
    initial = lax.slice_in_dim(value, 0, width, axis=dim).astype(LINK)
    return lax.ppermute(last, axis, up), lax.ppermute(initial, axis, down)


def halos_shared(value, width, dim):
    peers, pair = lax.axis_size("space"), lax.axis_size("batch")
    if pair % 2:
        return halos(value, "space", width, dim)
    length = value.shape[dim]
    odd = lax.axis_index("batch") % 2 == 1
    last = lax.slice_in_dim(value, length - width, length, axis=dim)
    initial = lax.slice_in_dim(value, 0, width, axis=dim)
    routes = []
    for s in range(peers):
        for b in range(pair):
            ahead = (s + 1) % peers if b % 2 == 0 else (s - 1) % peers
            routes.append((s * pair + b, ahead * pair + b))
    got = lax.ppermute(jnp.where(odd, initial, last).astype(LINK), ("space", "batch"), routes)
    other = lax.ppermute(got, "batch", [(b, b ^ 1) for b in range(pair)])
    return jnp.where(odd, other, got), jnp.where(odd, got, other)


ROWS = 256


def stencil_parts(flag_ref, x_ref, xb_ref, xa_ref, d_ref, v_ref, cb_ref, ca_ref, halo):
    planes, span, depth = x_ref.shape[1], x_ref.shape[2], x_ref.shape[3]
    block = math.gcd(span, ROWS)
    tiles = span // block
    sub = lax.broadcasted_iota(jnp.int32, (block, depth), 0)
    lane = lax.broadcasted_iota(jnp.int32, (block, depth), 1)

    def rows(c):
        return pl.ds(pl.multiple_of(c * block, block), block)

    def level0(k, c):
        if k < halo:
            return xb_ref[0, k, rows(c), :].astype(jnp.float32)
        if k < halo + planes:
            return x_ref[0, k - halo, rows(c), :]
        return xa_ref[0, k - halo - planes, rows(c), :].astype(jnp.float32)

    def coef(which, k, c):
        if k < halo:
            return cb_ref[which, k, rows(c), :].astype(jnp.float32)
        if k < halo + planes:
            return (d_ref if which == 0 else v_ref)[k - halo, rows(c), :]
        return ca_ref[which, k - halo - planes, rows(c), :].astype(jnp.float32)

    def lap(m, zero, p, before, after):
        total = p + m
        up = jnp.where(sub == block - 1, pltpu.roll(after, block - 1, 0), pltpu.roll(zero, block - 1, 0))
        down = jnp.where(sub == 0, pltpu.roll(before, 1, 0), pltpu.roll(zero, 1, 0))
        total = total + up + down
        zu = jnp.where(lane == depth - 1, 0.0, pltpu.roll(zero, depth - 1, 1))
        zd = jnp.where(lane == 0, 0.0, pltpu.roll(zero, 1, 1))
        total = total + zu + zd
        return total - 6.0 * zero

    def update(load, k, c, adjoint):
        prev, nxt = (c + tiles - 1) % tiles, (c + 1) % tiles
        xm, x0, xp = load(k - 1, c), load(k, c), load(k + 1, c)
        xbefore, xafter = load(k, prev), load(k, nxt)
        if adjoint:
            lifted = lap(coef(0, k - 1, c) * xm, coef(0, k, c) * x0, coef(0, k + 1, c) * xp,
                         coef(0, k, prev) * xbefore, coef(0, k, nxt) * xafter)
            slope = 0.5 * (coef(1, k + 1, c) * xp - coef(1, k - 1, c) * xm)
            return x0 + lifted + slope
        lifted = lap(xm, x0, xp, xbefore, xafter)
        slope = 0.5 * (xp - xm)
        return x0 + coef(0, k, c) * lifted - coef(1, k, c) * slope

    def store(ref, slot, c, value):
        quarter = ref.shape[3]
        per = block // quarter
        for j in range(per):
            ref[0, c * per + j, slot] = value[j * quarter:(j + 1) * quarter].astype(ref.dtype)

    def both(run):
        @pl.when(flag_ref[0] == 0)
        def _():
            run(False)

        @pl.when(flag_ref[0] != 0)
        def _():
            run(True)

    return planes, tiles, rows, level0, update, both, store


def interior_kernel(flag_ref, x_ref, d_ref, v_ref, s_ref):
    halo = STEPS
    planes, tiles, _, level0, update, both, store = stencil_parts(
        flag_ref, x_ref, None, None, d_ref, v_ref, None, None, halo)

    def run(adjoint):
        for k in range(halo + 1, halo + planes - 1):
            def first(c, carry, k=k):
                store(s_ref, k - halo - 1, c, update(level0, k, c, adjoint))
                return carry

            lax.fori_loop(0, tiles, first, 0, unroll=2)

    both(run)


def stencil_kernel(flag_ref, x_ref, xb_ref, xa_ref, d_ref, v_ref, cb_ref, ca_ref, out_ref, late_ref, mid_ref):
    halo = xb_ref.shape[1]
    planes, tiles, rows, level0, update, both, store = stencil_parts(
        flag_ref, x_ref, xb_ref, xa_ref, d_ref, v_ref, cb_ref, ca_ref, halo)
    ext = planes + 2 * halo

    def level1(k, c):
        return mid_ref[k - 1, rows(c), :]

    def run(adjoint):
        for k in range(1, ext - 1):
            def first(c, carry, k=k):
                value = update(level0, k, c, adjoint)
                mid_ref[k - 1, rows(c), :] = value
                if k == halo or k == halo + planes - 1:
                    store(late_ref, 0 if k == halo else 1, c, value)
                return carry

            lax.fori_loop(0, tiles, first, 0, unroll=2)
        for k in range(halo, halo + planes):
            def second(c, carry, k=k):
                value = update(level1, k, c, adjoint)
                out_ref[0, k - halo, rows(c), :] = value
                p = k - halo
                store(late_ref, 2 + (0 if p == 0 else 1 if p == planes - 1 else 1 + p), c, value)
                return carry

            lax.fori_loop(0, tiles, second, 0, unroll=2)

    both(run)


def interior_step(flag, state, diffusion, velocity, share):
    fields, planes, span, depth = state.shape
    return pl.pallas_call(
        interior_kernel,
        grid=(fields,),
        in_specs=[
            pl.BlockSpec(memory_space=pltpu.SMEM),
            pl.BlockSpec((1, planes, span, depth), lambda f: (f, 0, 0, 0)),
            pl.BlockSpec((planes, span, depth), lambda f: (0, 0, 0)),
            pl.BlockSpec((planes, span, depth), lambda f: (0, 0, 0)),
        ],
        out_specs=pl.BlockSpec((1, share, planes - 2, span // share, depth), lambda f: (f, 0, 0, 0, 0)),
        out_shape=jax.ShapeDtypeStruct((fields, share, planes - 2, span // share, depth), jnp.bfloat16),
        compiler_params=pltpu.CompilerParams(dimension_semantics=("arbitrary",)),
    )(flag, state, diffusion, velocity)


def two_steps(flag, state, before, after, diffusion, velocity, coef_before, coef_after, share):
    fields, planes, span, depth = state.shape
    halo = before.shape[1]
    field_block = lambda n: pl.BlockSpec((1, n, span, depth), lambda f: (f, 0, 0, 0))
    whole = lambda shape: pl.BlockSpec(shape, lambda f: (0,) * len(shape))
    return pl.pallas_call(
        stencil_kernel,
        grid=(fields,),
        in_specs=[
            pl.BlockSpec(memory_space=pltpu.SMEM),
            field_block(planes),
            field_block(halo),
            field_block(halo),
            whole((planes, span, depth)),
            whole((planes, span, depth)),
            whole((2, halo, span, depth)),
            whole((2, halo, span, depth)),
        ],
        out_specs=[
            field_block(planes),
            pl.BlockSpec((1, share, 2 + planes, span // share, depth), lambda f: (f, 0, 0, 0, 0)),
        ],
        out_shape=[
            jax.ShapeDtypeStruct(state.shape, jnp.float32),
            jax.ShapeDtypeStruct((fields, share, 2 + planes, span // share, depth), jnp.bfloat16),
        ],
        scratch_shapes=[pltpu.VMEM((planes + 2 * halo - 2, span, depth), jnp.float32)],
        compiler_params=pltpu.CompilerParams(dimension_semantics=("arbitrary",)),
    )(flag, state, before, after, diffusion, velocity, coef_before, coef_after)


def pieces(x):
    out, rest = [], x
    for _ in range(3):
        part = lax.reduce_precision(rest, exponent_bits=8, mantissa_bits=7)
        out.append(part.astype(jnp.bfloat16))
        rest = rest - part
    return out


def select(onehot, values):
    depth = values.shape[-1]
    parts = pieces(values)
    terms = jnp.einsum("fmk,fkd->fmd", onehot, jnp.concatenate(parts, axis=-1), preferred_element_type=jnp.float32)
    total = terms[..., :depth]
    for i in range(1, len(parts)):
        total = total + terms[..., i * depth:(i + 1) * depth]
    return total


def butterfly(value, axes):
    for axis in axes:
        n = lax.axis_size(axis)
        step = 1
        while step < n:
            value = value + lax.ppermute(value, axis, [(i, i ^ step) for i in range(n)])
            step *= 2
    return value


def work(owner, offset, profile, diffusion, velocity):
    count = lax.axis_size("space")
    fields_dev, rows_dev = offset.shape
    planes, span, depth = diffusion.shape
    cap = 4 * rows_dev // count
    slots = count * cap
    col_rows = -(-cap // depth)

    target = owner[..., 0]
    earlier = jnp.tril(jnp.ones((rows_dev, rows_dev), jnp.bool_), -1)
    same = target[:, :, None] == target[:, None, :]
    rank = jnp.sum(jnp.logical_and(same, earlier[None]), axis=2)
    slot = target * cap + rank
    hit = slot[:, None, :] == lax.broadcasted_iota(jnp.int32, (fields_dev, slots, rows_dev), 1)
    send_vals = select(hit.astype(jnp.bfloat16), profile)
    send_cols = jnp.sum(jnp.where(hit, offset[:, None, :], 0), axis=2).astype(jnp.float32)
    send_cols = jnp.pad(send_cols.reshape(fields_dev, count, cap), ((0, 0), (0, 0), (0, col_rows * depth - cap)))
    payload = jnp.concatenate(
        [send_vals.reshape(fields_dev, count, cap, depth), send_cols.reshape(fields_dev, count, col_rows, depth)],
        axis=2,
    )
    got = lax.all_to_all(payload, "space", split_axis=1, concat_axis=1, tiled=True)
    got_vals = got[:, :, :cap].reshape(fields_dev, slots, depth)
    got_cols = got[:, :, cap:].reshape(fields_dev, count, col_rows * depth)[:, :, :cap]
    got_cols = got_cols.reshape(fields_dev, slots).astype(jnp.int32)

    place = got_cols[:, None, :] == lax.broadcasted_iota(jnp.int32, (fields_dev, planes * span, slots), 1)
    state = select(place.astype(jnp.bfloat16), got_vals).reshape(fields_dev, planes, span, depth)

    adjoint = lax.axis_index("batch") >= lax.axis_size("batch") // 2
    flag = adjoint.astype(jnp.int32).reshape(1)
    coef_before, coef_after = halos_shared(jnp.stack([diffusion, velocity]), STEPS, 1)
    share = lax.axis_size("batch")
    inner = interior_step(flag, state, diffusion, velocity, share)
    before, after = halos(state, "space", STEPS, 1)
    state, late = two_steps(flag, state, before, after, diffusion, velocity, coef_before, coef_after, share)

    def spread(snap):
        mixed = lax.all_to_all(snap, "batch", split_axis=1, concat_axis=0, tiled=True)
        return mixed.reshape(mixed.shape[0], mixed.shape[2], -1)

    inner, late = spread(inner), spread(late)
    snaps = [(late[:, 0:2], inner), (late[:, 2:4], late[:, 4:])]
    rows = []
    for sensed in snaps:
        row = []
        for actuated in snaps:
            block = None
            for s_part, a_part in zip(sensed, actuated):
                term = lax.dot_general(
                    s_part[ACT:ACT + SENS].reshape(SENS, -1), a_part[:ACT].reshape(ACT, -1),
                    (((1,), (1,)), ((), ())), preferred_element_type=jnp.float32,
                )
                block = term if block is None else block + term
            row.append(block)
        rows.append(jnp.concatenate(row, axis=1))
    partial_gram = jnp.concatenate(rows, axis=0)
    scale = 4.0 / math.sqrt(planes * count * span * depth)
    gram = butterfly(partial_gram, ("batch", "space")) * scale
    return (state, gram)


def solution(mesh):
    in_specs = (
        P("batch", "space", None),
        P("batch", "space"),
        P("batch", "space", None),
        P("space", None, None),
        P("space", None, None),
    )
    out_specs = (P("batch", "space", None, None), P())
    return jax.shard_map(work, mesh=mesh, in_specs=in_specs, out_specs=out_specs, check_vma=False)
```

```python
import math

import jax
import jax.numpy as jnp
from jax import lax
from jax.experimental import pallas as pl
from jax.experimental.pallas import tpu as pltpu
from jax.sharding import PartitionSpec as P

STEPS = 2
ACT = 4
SENS = 4


LINK = jnp.bfloat16


def halos(value, axis, width, dim):
    peers, length = lax.axis_size(axis), value.shape[dim]
    up = [(i, (i + 1) % peers) for i in range(peers)]
    down = [(j, i) for i, j in up]
    last = lax.slice_in_dim(value, length - width, length, axis=dim).astype(LINK)
    initial = lax.slice_in_dim(value, 0, width, axis=dim).astype(LINK)
    return lax.ppermute(last, axis, up), lax.ppermute(initial, axis, down)


def halos_shared(value, width, dim):
    peers, pair = lax.axis_size("space"), lax.axis_size("batch")
    if pair % 2:
        return halos(value, "space", width, dim)
    length = value.shape[dim]
    odd = lax.axis_index("batch") % 2 == 1
    last = lax.slice_in_dim(value, length - width, length, axis=dim)
    initial = lax.slice_in_dim(value, 0, width, axis=dim)
    routes = []
    for s in range(peers):
        for b in range(pair):
            ahead = (s + 1) % peers if b % 2 == 0 else (s - 1) % peers
            routes.append((s * pair + b, ahead * pair + b))
    got = lax.ppermute(jnp.where(odd, initial, last).astype(LINK), ("space", "batch"), routes)
    other = lax.ppermute(got, "batch", [(b, b ^ 1) for b in range(pair)])
    return jnp.where(odd, other, got), jnp.where(odd, got, other)


ROWS = 256


def stencil_parts(flag_ref, x_ref, xb_ref, xa_ref, d_ref, v_ref, cb_ref, ca_ref, halo):
    planes, span, depth = x_ref.shape[1], x_ref.shape[2], x_ref.shape[3]
    block = math.gcd(span, ROWS)
    tiles = span // block
    sub = lax.broadcasted_iota(jnp.int32, (block, depth), 0)
    lane = lax.broadcasted_iota(jnp.int32, (block, depth), 1)

    def rows(c):
        return pl.ds(pl.multiple_of(c * block, block), block)

    def level0(k, c):
        if k < halo:
            return xb_ref[0, k, rows(c), :].astype(jnp.float32)
        if k < halo + planes:
            return x_ref[0, k - halo, rows(c), :]
        return xa_ref[0, k - halo - planes, rows(c), :].astype(jnp.float32)

    def coef(which, k, c):
        if k < halo:
            return cb_ref[which, k, rows(c), :].astype(jnp.float32)
        if k < halo + planes:
            return (d_ref if which == 0 else v_ref)[k - halo, rows(c), :]
        return ca_ref[which, k - halo - planes, rows(c), :].astype(jnp.float32)

    def lap(m, zero, p, before, after):
        total = p + m
        up = jnp.where(sub == block - 1, pltpu.roll(after, block - 1, 0), pltpu.roll(zero, block - 1, 0))
        down = jnp.where(sub == 0, pltpu.roll(before, 1, 0), pltpu.roll(zero, 1, 0))
        total = total + up + down
        zu = jnp.where(lane == depth - 1, 0.0, pltpu.roll(zero, depth - 1, 1))
        zd = jnp.where(lane == 0, 0.0, pltpu.roll(zero, 1, 1))
        total = total + zu + zd
        return total - 6.0 * zero

    def update(load, k, c, adjoint):
        prev, nxt = (c + tiles - 1) % tiles, (c + 1) % tiles
        xm, x0, xp = load(k - 1, c), load(k, c), load(k + 1, c)
        xbefore, xafter = load(k, prev), load(k, nxt)
        if adjoint:
            lifted = lap(coef(0, k - 1, c) * xm, coef(0, k, c) * x0, coef(0, k + 1, c) * xp,
                         coef(0, k, prev) * xbefore, coef(0, k, nxt) * xafter)
            slope = 0.5 * (coef(1, k + 1, c) * xp - coef(1, k - 1, c) * xm)
            return x0 + lifted + slope
        lifted = lap(xm, x0, xp, xbefore, xafter)
        slope = 0.5 * (xp - xm)
        return x0 + coef(0, k, c) * lifted - coef(1, k, c) * slope

    def store(ref, slot, c, value):
        quarter = ref.shape[3]
        per = block // quarter
        for j in range(per):
            ref[c * per + j, 0, slot] = value[j * quarter:(j + 1) * quarter].astype(ref.dtype)

    def both(run):
        @pl.when(flag_ref[0] == 0)
        def _():
            run(False)

        @pl.when(flag_ref[0] != 0)
        def _():
            run(True)

    return planes, tiles, rows, level0, update, both, store


def interior_kernel(flag_ref, x_ref, d_ref, v_ref, s_ref):
    halo = STEPS
    planes, tiles, _, level0, update, both, store = stencil_parts(
        flag_ref, x_ref, None, None, d_ref, v_ref, None, None, halo)

    def run(adjoint):
        for k in range(halo + 1, halo + planes - 1):
            def first(c, carry, k=k):
                store(s_ref, k - halo - 1, c, update(level0, k, c, adjoint))
                return carry

            lax.fori_loop(0, tiles, first, 0, unroll=2)

    both(run)


def stencil_kernel(flag_ref, x_ref, xb_ref, xa_ref, d_ref, v_ref, cb_ref, ca_ref, out_ref, late_ref, mid_ref):
    halo = xb_ref.shape[1]
    planes, tiles, rows, level0, update, both, store = stencil_parts(
        flag_ref, x_ref, xb_ref, xa_ref, d_ref, v_ref, cb_ref, ca_ref, halo)
    ext = planes + 2 * halo

    def level1(k, c):
        return mid_ref[k - 1, rows(c), :]

    def run(adjoint):
        for k in range(1, ext - 1):
            def first(c, carry, k=k):
                value = update(level0, k, c, adjoint)
                mid_ref[k - 1, rows(c), :] = value
                if k == halo or k == halo + planes - 1:
                    store(late_ref, 0 if k == halo else 1, c, value)
                return carry

            lax.fori_loop(0, tiles, first, 0, unroll=2)
        for k in range(halo, halo + planes):
            def second(c, carry, k=k):
                value = update(level1, k, c, adjoint)
                out_ref[0, k - halo, rows(c), :] = value
                p = k - halo
                store(late_ref, 2 + (0 if p == 0 else 1 if p == planes - 1 else 1 + p), c, value)
                return carry

            lax.fori_loop(0, tiles, second, 0, unroll=2)

    both(run)


def interior_step(flag, state, diffusion, velocity, share):
    fields, planes, span, depth = state.shape
    return pl.pallas_call(
        interior_kernel,
        grid=(fields,),
        in_specs=[
            pl.BlockSpec(memory_space=pltpu.SMEM),
            pl.BlockSpec((1, planes, span, depth), lambda f: (f, 0, 0, 0)),
            pl.BlockSpec((planes, span, depth), lambda f: (0, 0, 0)),
            pl.BlockSpec((planes, span, depth), lambda f: (0, 0, 0)),
        ],
        out_specs=pl.BlockSpec((share, 1, planes - 2, span // share, depth), lambda f: (0, f, 0, 0, 0)),
        out_shape=jax.ShapeDtypeStruct((share, fields, planes - 2, span // share, depth), jnp.bfloat16),
        compiler_params=pltpu.CompilerParams(dimension_semantics=("arbitrary",)),
    )(flag, state, diffusion, velocity)


def two_steps(flag, state, before, after, diffusion, velocity, coef_before, coef_after, share):
    fields, planes, span, depth = state.shape
    halo = before.shape[1]
    field_block = lambda n: pl.BlockSpec((1, n, span, depth), lambda f: (f, 0, 0, 0))
    whole = lambda shape: pl.BlockSpec(shape, lambda f: (0,) * len(shape))
    return pl.pallas_call(
        stencil_kernel,
        grid=(fields,),
        in_specs=[
            pl.BlockSpec(memory_space=pltpu.SMEM),
            field_block(planes),
            field_block(halo),
            field_block(halo),
            whole((planes, span, depth)),
            whole((planes, span, depth)),
            whole((2, halo, span, depth)),
            whole((2, halo, span, depth)),
        ],
        out_specs=[
            field_block(planes),
            pl.BlockSpec((share, 1, 2 + planes, span // share, depth), lambda f: (0, f, 0, 0, 0)),
        ],
        out_shape=[
            jax.ShapeDtypeStruct(state.shape, jnp.float32),
            jax.ShapeDtypeStruct((share, fields, 2 + planes, span // share, depth), jnp.bfloat16),
        ],
        scratch_shapes=[pltpu.VMEM((planes + 2 * halo - 2, span, depth), jnp.float32)],
        compiler_params=pltpu.CompilerParams(dimension_semantics=("arbitrary",)),
    )(flag, state, before, after, diffusion, velocity, coef_before, coef_after)


def pieces(x):
    out, rest = [], x
    for _ in range(3):
        part = lax.reduce_precision(rest, exponent_bits=8, mantissa_bits=7)
        out.append(part.astype(jnp.bfloat16))
        rest = rest - part
    return out


def select(onehot, values):
    depth = values.shape[-1]
    parts = pieces(values)
    terms = jnp.einsum("fmk,fkd->fmd", onehot, jnp.concatenate(parts, axis=-1), preferred_element_type=jnp.float32)
    total = terms[..., :depth]
    for i in range(1, len(parts)):
        total = total + terms[..., i * depth:(i + 1) * depth]
    return total


def butterfly(value, axes):
    for axis in axes:
        n = lax.axis_size(axis)
        step = 1
        while step < n:
            value = value + lax.ppermute(value, axis, [(i, i ^ step) for i in range(n)])
            step *= 2
    return value


def work(owner, offset, profile, diffusion, velocity):
    count = lax.axis_size("space")
    fields_dev, rows_dev = offset.shape
    planes, span, depth = diffusion.shape
    cap = 4 * rows_dev // count
    slots = count * cap
    col_rows = -(-cap // depth)

    target = owner[..., 0]
    earlier = jnp.tril(jnp.ones((rows_dev, rows_dev), jnp.bool_), -1)
    same = target[:, :, None] == target[:, None, :]
    rank = jnp.sum(jnp.logical_and(same, earlier[None]), axis=2)
    slot = target * cap + rank
    hit = slot[:, None, :] == lax.broadcasted_iota(jnp.int32, (fields_dev, slots, rows_dev), 1)
    send_vals = select(hit.astype(jnp.bfloat16), profile)
    send_cols = jnp.sum(jnp.where(hit, offset[:, None, :], 0), axis=2).astype(jnp.float32)
    send_cols = jnp.pad(send_cols.reshape(fields_dev, count, cap), ((0, 0), (0, 0), (0, col_rows * depth - cap)))
    payload = jnp.concatenate(
        [send_vals.reshape(fields_dev, count, cap, depth), send_cols.reshape(fields_dev, count, col_rows, depth)],
        axis=2,
    )
    got = lax.all_to_all(payload, "space", split_axis=1, concat_axis=1, tiled=True)
    got_vals = got[:, :, :cap].reshape(fields_dev, slots, depth)
    got_cols = got[:, :, cap:].reshape(fields_dev, count, col_rows * depth)[:, :, :cap]
    got_cols = got_cols.reshape(fields_dev, slots).astype(jnp.int32)

    place = got_cols[:, None, :] == lax.broadcasted_iota(jnp.int32, (fields_dev, planes * span, slots), 1)
    state = select(place.astype(jnp.bfloat16), got_vals).reshape(fields_dev, planes, span, depth)

    adjoint = lax.axis_index("batch") >= lax.axis_size("batch") // 2
    flag = adjoint.astype(jnp.int32).reshape(1)
    coef_before, coef_after = halos_shared(jnp.stack([diffusion, velocity]), STEPS, 1)
    share = lax.axis_size("batch")
    inner = interior_step(flag, state, diffusion, velocity, share)
    before, after = halos(state, "space", STEPS, 1)
    state, late = two_steps(flag, state, before, after, diffusion, velocity, coef_before, coef_after, share)

    def spread(snap):
        mixed = lax.all_to_all(snap, "batch", split_axis=0, concat_axis=0, tiled=True)
        return mixed.reshape(mixed.shape[0] * mixed.shape[1], mixed.shape[2], -1)

    inner, late = spread(inner), spread(late)
    snaps = [(late[:, 0:2], inner), (late[:, 2:4], late[:, 4:])]
    rows = []
    for sensed in snaps:
        row = []
        for actuated in snaps:
            block = None
            for s_part, a_part in zip(sensed, actuated):
                term = lax.dot_general(
                    s_part[ACT:ACT + SENS].reshape(SENS, -1), a_part[:ACT].reshape(ACT, -1),
                    (((1,), (1,)), ((), ())), preferred_element_type=jnp.float32,
                )
                block = term if block is None else block + term
            row.append(block)
        rows.append(jnp.concatenate(row, axis=1))
    partial_gram = jnp.concatenate(rows, axis=0)
    scale = 4.0 / math.sqrt(planes * count * span * depth)
    gram = butterfly(partial_gram, ("batch", "space")) * scale
    return (state, gram)


def solution(mesh):
    in_specs = (
        P("batch", "space", None),
        P("batch", "space"),
        P("batch", "space", None),
        P("space", None, None),
        P("space", None, None),
    )
    out_specs = (P("batch", "space", None, None), P())
    return jax.shard_map(work, mesh=mesh, in_specs=in_specs, out_specs=out_specs, check_vma=False)
```

```python
import math

import jax
import jax.numpy as jnp
from jax import lax
from jax.experimental import pallas as pl
from jax.experimental.pallas import tpu as pltpu
from jax.sharding import PartitionSpec as P

STEPS = 2
ACT = 4
SENS = 4


LINK = jnp.bfloat16


def halos(value, axis, width, dim):
    peers, length = lax.axis_size(axis), value.shape[dim]
    up = [(i, (i + 1) % peers) for i in range(peers)]
    down = [(j, i) for i, j in up]
    last = lax.slice_in_dim(value, length - width, length, axis=dim).astype(LINK)
    initial = lax.slice_in_dim(value, 0, width, axis=dim).astype(LINK)
    return lax.ppermute(last, axis, up), lax.ppermute(initial, axis, down)


def halos_shared(value, width, dim):
    peers, pair = lax.axis_size("space"), lax.axis_size("batch")
    if pair % 4 or value.shape[0] != 2:
        return halos(value, "space", width, dim)
    length = value.shape[dim]
    index = lax.axis_index("batch")
    upper = index % 2 == 1
    second = (index // 2) % 2 == 1
    last = lax.slice_in_dim(value, length - width, length, axis=dim)
    initial = lax.slice_in_dim(value, 0, width, axis=dim)
    side = jnp.where(upper, initial, last)
    routes = []
    for s in range(peers):
        for b in range(pair):
            ahead = (s + 1) % peers if b % 2 == 0 else (s - 1) % peers
            routes.append((s * pair + b, ahead * pair + b))
    got = lax.ppermute(jnp.where(second, side[1], side[0]).astype(LINK), ("space", "batch"), routes)
    other = lax.ppermute(got, "batch", [(b, b ^ 1) for b in range(pair)])
    mine = jnp.stack([jnp.where(upper, other, got), jnp.where(upper, got, other)])
    theirs = lax.ppermute(mine, "batch", [(b, b ^ 2) for b in range(pair)])
    first_coef = jnp.where(second, theirs, mine)
    second_coef = jnp.where(second, mine, theirs)
    return jnp.stack([first_coef[0], second_coef[0]]), jnp.stack([first_coef[1], second_coef[1]])


ROWS = 256


def stencil_parts(flag_ref, x_ref, xb_ref, xa_ref, d_ref, v_ref, cb_ref, ca_ref, halo):
    planes, span, depth = x_ref.shape[1], x_ref.shape[2], x_ref.shape[3]
    block = math.gcd(span, ROWS)
    tiles = span // block
    sub = lax.broadcasted_iota(jnp.int32, (block, depth), 0)
    lane = lax.broadcasted_iota(jnp.int32, (block, depth), 1)

    def rows(c):
        return pl.ds(pl.multiple_of(c * block, block), block)

    def level0(k, c):
        if k < halo:
            return xb_ref[0, k, rows(c), :].astype(jnp.float32)
        if k < halo + planes:
            return x_ref[0, k - halo, rows(c), :]
        return xa_ref[0, k - halo - planes, rows(c), :].astype(jnp.float32)

    def coef(which, k, c):
        if k < halo:
            return cb_ref[which, k, rows(c), :].astype(jnp.float32)
        if k < halo + planes:
            return (d_ref if which == 0 else v_ref)[k - halo, rows(c), :]
        return ca_ref[which, k - halo - planes, rows(c), :].astype(jnp.float32)

    def lap(m, zero, p, before, after):
        total = p + m
        up = jnp.where(sub == block - 1, pltpu.roll(after, block - 1, 0), pltpu.roll(zero, block - 1, 0))
        down = jnp.where(sub == 0, pltpu.roll(before, 1, 0), pltpu.roll(zero, 1, 0))
        total = total + up + down
        zu = jnp.where(lane == depth - 1, 0.0, pltpu.roll(zero, depth - 1, 1))
        zd = jnp.where(lane == 0, 0.0, pltpu.roll(zero, 1, 1))
        total = total + zu + zd
        return total - 6.0 * zero

    def update(load, k, c, adjoint):
        prev, nxt = (c + tiles - 1) % tiles, (c + 1) % tiles
        xm, x0, xp = load(k - 1, c), load(k, c), load(k + 1, c)
        xbefore, xafter = load(k, prev), load(k, nxt)
        if adjoint:
            lifted = lap(coef(0, k - 1, c) * xm, coef(0, k, c) * x0, coef(0, k + 1, c) * xp,
                         coef(0, k, prev) * xbefore, coef(0, k, nxt) * xafter)
            slope = 0.5 * (coef(1, k + 1, c) * xp - coef(1, k - 1, c) * xm)
            return x0 + lifted + slope
        lifted = lap(xm, x0, xp, xbefore, xafter)
        slope = 0.5 * (xp - xm)
        return x0 + coef(0, k, c) * lifted - coef(1, k, c) * slope

    def store(ref, slot, c, value):
        quarter = ref.shape[3]
        per = block // quarter
        for j in range(per):
            ref[c * per + j, 0, slot] = value[j * quarter:(j + 1) * quarter].astype(ref.dtype)

    def both(run):
        @pl.when(flag_ref[0] == 0)
        def _():
            run(False)

        @pl.when(flag_ref[0] != 0)
        def _():
            run(True)

    return planes, tiles, rows, level0, update, both, store


def interior_kernel(flag_ref, x_ref, d_ref, v_ref, s_ref):
    halo = STEPS
    planes, tiles, _, level0, update, both, store = stencil_parts(
        flag_ref, x_ref, None, None, d_ref, v_ref, None, None, halo)

    def run(adjoint):
        for k in range(halo + 1, halo + planes - 1):
            def first(c, carry, k=k):
                store(s_ref, k - halo - 1, c, update(level0, k, c, adjoint))
                return carry

            lax.fori_loop(0, tiles, first, 0, unroll=2)

    both(run)


def stencil_kernel(flag_ref, x_ref, xb_ref, xa_ref, d_ref, v_ref, cb_ref, ca_ref, out_ref, late_ref, mid_ref):
    halo = xb_ref.shape[1]
    planes, tiles, rows, level0, update, both, store = stencil_parts(
        flag_ref, x_ref, xb_ref, xa_ref, d_ref, v_ref, cb_ref, ca_ref, halo)
    ext = planes + 2 * halo

    def level1(k, c):
        return mid_ref[k - 1, rows(c), :]

    def run(adjoint):
        for k in range(1, ext - 1):
            def first(c, carry, k=k):
                value = update(level0, k, c, adjoint)
                mid_ref[k - 1, rows(c), :] = value
                if k == halo or k == halo + planes - 1:
                    store(late_ref, 0 if k == halo else 1, c, value)
                return carry

            lax.fori_loop(0, tiles, first, 0, unroll=2)
        for k in range(halo, halo + planes):
            def second(c, carry, k=k):
                value = update(level1, k, c, adjoint)
                out_ref[0, k - halo, rows(c), :] = value
                p = k - halo
                store(late_ref, 2 + (0 if p == 0 else 1 if p == planes - 1 else 1 + p), c, value)
                return carry

            lax.fori_loop(0, tiles, second, 0, unroll=2)

    both(run)


def interior_step(flag, state, diffusion, velocity, share):
    fields, planes, span, depth = state.shape
    return pl.pallas_call(
        interior_kernel,
        grid=(fields,),
        in_specs=[
            pl.BlockSpec(memory_space=pltpu.SMEM),
            pl.BlockSpec((1, planes, span, depth), lambda f: (f, 0, 0, 0)),
            pl.BlockSpec((planes, span, depth), lambda f: (0, 0, 0)),
            pl.BlockSpec((planes, span, depth), lambda f: (0, 0, 0)),
        ],
        out_specs=pl.BlockSpec((share, 1, planes - 2, span // share, depth), lambda f: (0, f, 0, 0, 0)),
        out_shape=jax.ShapeDtypeStruct((share, fields, planes - 2, span // share, depth), jnp.bfloat16),
        compiler_params=pltpu.CompilerParams(dimension_semantics=("arbitrary",)),
    )(flag, state, diffusion, velocity)


def two_steps(flag, state, before, after, diffusion, velocity, coef_before, coef_after, share):
    fields, planes, span, depth = state.shape
    halo = before.shape[1]
    field_block = lambda n: pl.BlockSpec((1, n, span, depth), lambda f: (f, 0, 0, 0))
    whole = lambda shape: pl.BlockSpec(shape, lambda f: (0,) * len(shape))
    return pl.pallas_call(
        stencil_kernel,
        grid=(fields,),
        in_specs=[
            pl.BlockSpec(memory_space=pltpu.SMEM),
            field_block(planes),
            field_block(halo),
            field_block(halo),
            whole((planes, span, depth)),
            whole((planes, span, depth)),
            whole((2, halo, span, depth)),
            whole((2, halo, span, depth)),
        ],
        out_specs=[
            field_block(planes),
            pl.BlockSpec((share, 1, 2 + planes, span // share, depth), lambda f: (0, f, 0, 0, 0)),
        ],
        out_shape=[
            jax.ShapeDtypeStruct(state.shape, jnp.float32),
            jax.ShapeDtypeStruct((share, fields, 2 + planes, span // share, depth), jnp.bfloat16),
        ],
        scratch_shapes=[pltpu.VMEM((planes + 2 * halo - 2, span, depth), jnp.float32)],
        compiler_params=pltpu.CompilerParams(dimension_semantics=("arbitrary",)),
    )(flag, state, before, after, diffusion, velocity, coef_before, coef_after)


def pieces(x):
    out, rest = [], x
    for _ in range(2):
        part = lax.reduce_precision(rest, exponent_bits=8, mantissa_bits=7)
        out.append(part.astype(jnp.bfloat16))
        rest = rest - part
    return out


def select(onehot, values):
    depth = values.shape[-1]
    parts = pieces(values)
    terms = jnp.einsum("fmk,fkd->fmd", onehot, jnp.concatenate(parts, axis=-1), preferred_element_type=jnp.float32)
    total = terms[..., :depth]
    for i in range(1, len(parts)):
        total = total + terms[..., i * depth:(i + 1) * depth]
    return total


def butterfly(value, axes):
    for axis in axes:
        n = lax.axis_size(axis)
        step = 1
        while step < n:
            value = value + lax.ppermute(value, axis, [(i, i ^ step) for i in range(n)])
            step *= 2
    return value


def work(owner, offset, profile, diffusion, velocity):
    count = lax.axis_size("space")
    fields_dev, rows_dev = offset.shape
    planes, span, depth = diffusion.shape
    cap = 4 * rows_dev // count
    slots = count * cap
    col_rows = -(-cap // depth)

    target = owner[..., 0]
    earlier = jnp.tril(jnp.ones((rows_dev, rows_dev), jnp.bool_), -1)
    same = target[:, :, None] == target[:, None, :]
    rank = jnp.sum(jnp.logical_and(same, earlier[None]), axis=2)
    slot = target * cap + rank
    hit = slot[:, None, :] == lax.broadcasted_iota(jnp.int32, (fields_dev, slots, rows_dev), 1)
    send_vals = select(hit.astype(jnp.bfloat16), profile)
    send_cols = jnp.sum(jnp.where(hit, offset[:, None, :], 0), axis=2).astype(jnp.float32)
    send_cols = jnp.pad(send_cols.reshape(fields_dev, count, cap), ((0, 0), (0, 0), (0, col_rows * depth - cap)))
    payload = jnp.concatenate(
        [send_vals.reshape(fields_dev, count, cap, depth), send_cols.reshape(fields_dev, count, col_rows, depth)],
        axis=2,
    )
    got = lax.all_to_all(payload, "space", split_axis=1, concat_axis=1, tiled=True)
    got_vals = got[:, :, :cap].reshape(fields_dev, slots, depth)
    got_cols = got[:, :, cap:].reshape(fields_dev, count, col_rows * depth)[:, :, :cap]
    got_cols = got_cols.reshape(fields_dev, slots).astype(jnp.int32)

    place = got_cols[:, None, :] == lax.broadcasted_iota(jnp.int32, (fields_dev, planes * span, slots), 1)
    state = select(place.astype(jnp.bfloat16), got_vals).reshape(fields_dev, planes, span, depth)

    adjoint = lax.axis_index("batch") >= lax.axis_size("batch") // 2
    flag = adjoint.astype(jnp.int32).reshape(1)
    coef_before, coef_after = halos_shared(jnp.stack([diffusion, velocity]), STEPS, 1)
    share = lax.axis_size("batch")
    inner = interior_step(flag, state, diffusion, velocity, share)
    before, after = halos(state, "space", STEPS, 1)
    state, late = two_steps(flag, state, before, after, diffusion, velocity, coef_before, coef_after, share)

    def spread(snap):
        mixed = lax.all_to_all(snap, "batch", split_axis=0, concat_axis=0, tiled=True)
        return mixed.reshape(mixed.shape[0] * mixed.shape[1], mixed.shape[2], -1)

    inner, late = spread(inner), spread(late)
    snaps = [(late[:, 0:2], inner), (late[:, 2:4], late[:, 4:])]
    rows = []
    for sensed in snaps:
        row = []
        for actuated in snaps:
            block = None
            for s_part, a_part in zip(sensed, actuated):
                term = lax.dot_general(
                    s_part[ACT:ACT + SENS].reshape(SENS, -1), a_part[:ACT].reshape(ACT, -1),
                    (((1,), (1,)), ((), ())), preferred_element_type=jnp.float32,
                )
                block = term if block is None else block + term
            row.append(block)
        rows.append(jnp.concatenate(row, axis=1))
    partial_gram = jnp.concatenate(rows, axis=0)
    scale = 4.0 / math.sqrt(planes * count * span * depth)
    gram = butterfly(partial_gram, ("batch", "space")) * scale
    return (state, gram)


def solution(mesh):
    in_specs = (
        P("batch", "space", None),
        P("batch", "space"),
        P("batch", "space", None),
        P("space", None, None),
        P("space", None, None),
    )
    out_specs = (P("batch", "space", None, None), P())
    return jax.shard_map(work, mesh=mesh, in_specs=in_specs, out_specs=out_specs, check_vma=False)
```

```python
import math

import jax
import jax.numpy as jnp
from jax import lax
from jax.experimental import pallas as pl
from jax.experimental.pallas import tpu as pltpu
from jax.sharding import PartitionSpec as P

STEPS = 2
ACT = 4
SENS = 4


LINK = jnp.bfloat16


def halos(value, axis, width, dim):
    peers, length = lax.axis_size(axis), value.shape[dim]
    up = [(i, (i + 1) % peers) for i in range(peers)]
    down = [(j, i) for i, j in up]
    last = lax.slice_in_dim(value, length - width, length, axis=dim).astype(LINK)
    initial = lax.slice_in_dim(value, 0, width, axis=dim).astype(LINK)
    return lax.ppermute(last, axis, up), lax.ppermute(initial, axis, down)


def halos_shared(value, width, dim):
    peers, pair = lax.axis_size("space"), lax.axis_size("batch")
    if pair % 2:
        return halos(value, "space", width, dim)
    length = value.shape[dim]
    odd = lax.axis_index("batch") % 2 == 1
    last = lax.slice_in_dim(value, length - width, length, axis=dim)
    initial = lax.slice_in_dim(value, 0, width, axis=dim)
    routes = []
    for s in range(peers):
        for b in range(pair):
            ahead = (s + 1) % peers if b % 2 == 0 else (s - 1) % peers
            routes.append((s * pair + b, ahead * pair + b))
    got = lax.ppermute(jnp.where(odd, initial, last).astype(LINK), ("space", "batch"), routes)
    other = lax.ppermute(got, "batch", [(b, b ^ 1) for b in range(pair)])
    return jnp.where(odd, other, got), jnp.where(odd, got, other)


ROWS = 256


def stencil_parts(flag_ref, x_ref, xb_ref, xa_ref, d_ref, v_ref, cb_ref, ca_ref, halo):
    planes, span, depth = x_ref.shape[1], x_ref.shape[2], x_ref.shape[3]
    block = math.gcd(span, ROWS)
    tiles = span // block
    sub = lax.broadcasted_iota(jnp.int32, (block, depth), 0)
    lane = lax.broadcasted_iota(jnp.int32, (block, depth), 1)

    def rows(c):
        return pl.ds(pl.multiple_of(c * block, block), block)

    def level0(k, c):
        if k < halo:
            return xb_ref[0, k, rows(c), :].astype(jnp.float32)
        if k < halo + planes:
            return x_ref[0, k - halo, rows(c), :]
        return xa_ref[0, k - halo - planes, rows(c), :].astype(jnp.float32)

    def coef(which, k, c):
        if k < halo:
            return cb_ref[which, k, rows(c), :].astype(jnp.float32)
        if k < halo + planes:
            return (d_ref if which == 0 else v_ref)[k - halo, rows(c), :]
        return ca_ref[which, k - halo - planes, rows(c), :].astype(jnp.float32)

    def lap(m, zero, p, before, after):
        total = p + m
        up = jnp.where(sub == block - 1, pltpu.roll(after, block - 1, 0), pltpu.roll(zero, block - 1, 0))
        down = jnp.where(sub == 0, pltpu.roll(before, 1, 0), pltpu.roll(zero, 1, 0))
        total = total + up + down
        zu = jnp.where(lane == depth - 1, 0.0, pltpu.roll(zero, depth - 1, 1))
        zd = jnp.where(lane == 0, 0.0, pltpu.roll(zero, 1, 1))
        total = total + zu + zd
        return total - 6.0 * zero

    def update(load, k, c, adjoint):
        prev, nxt = (c + tiles - 1) % tiles, (c + 1) % tiles
        xm, x0, xp = load(k - 1, c), load(k, c), load(k + 1, c)
        xbefore, xafter = load(k, prev), load(k, nxt)
        if adjoint:
            lifted = lap(coef(0, k - 1, c) * xm, coef(0, k, c) * x0, coef(0, k + 1, c) * xp,
                         coef(0, k, prev) * xbefore, coef(0, k, nxt) * xafter)
            slope = 0.5 * (coef(1, k + 1, c) * xp - coef(1, k - 1, c) * xm)
            return x0 + lifted + slope
        lifted = lap(xm, x0, xp, xbefore, xafter)
        slope = 0.5 * (xp - xm)
        return x0 + coef(0, k, c) * lifted - coef(1, k, c) * slope

    def store(ref, slot, c, value):
        quarter = ref.shape[3]
        per = block // quarter
        for j in range(per):
            ref[c * per + j, 0, slot] = value[j * quarter:(j + 1) * quarter].astype(ref.dtype)

    def both(run):
        @pl.when(flag_ref[0] == 0)
        def _():
            run(False)

        @pl.when(flag_ref[0] != 0)
        def _():
            run(True)

    return planes, tiles, rows, level0, update, both, store


def interior_kernel(flag_ref, x_ref, d_ref, v_ref, s_ref):
    halo = STEPS
    planes, tiles, _, level0, update, both, store = stencil_parts(
        flag_ref, x_ref, None, None, d_ref, v_ref, None, None, halo)

    def run(adjoint):
        for k in range(halo + 1, halo + planes - 1):
            def first(c, carry, k=k):
                store(s_ref, k - halo - 1, c, update(level0, k, c, adjoint))
                return carry

            lax.fori_loop(0, tiles, first, 0, unroll=2)

    both(run)


def stencil_kernel(flag_ref, x_ref, xb_ref, xa_ref, d_ref, v_ref, cb_ref, ca_ref, out_ref, late_ref, mid_ref):
    halo = xb_ref.shape[1]
    planes, tiles, rows, level0, update, both, store = stencil_parts(
        flag_ref, x_ref, xb_ref, xa_ref, d_ref, v_ref, cb_ref, ca_ref, halo)
    ext = planes + 2 * halo

    def level1(k, c):
        return mid_ref[k - 1, rows(c), :]

    def run(adjoint):
        for k in range(1, ext - 1):
            def first(c, carry, k=k):
                value = update(level0, k, c, adjoint)
                mid_ref[k - 1, rows(c), :] = value
                if k == halo or k == halo + planes - 1:
                    store(late_ref, 0 if k == halo else 1, c, value)
                return carry

            lax.fori_loop(0, tiles, first, 0, unroll=2)
        for k in range(halo, halo + planes):
            def second(c, carry, k=k):
                value = update(level1, k, c, adjoint)
                out_ref[0, k - halo, rows(c), :] = value
                p = k - halo
                store(late_ref, 2 + (0 if p == 0 else 1 if p == planes - 1 else 1 + p), c, value)
                return carry

            lax.fori_loop(0, tiles, second, 0, unroll=2)

    both(run)


def interior_step(flag, state, diffusion, velocity, share):
    fields, planes, span, depth = state.shape
    return pl.pallas_call(
        interior_kernel,
        grid=(fields,),
        in_specs=[
            pl.BlockSpec(memory_space=pltpu.SMEM),
            pl.BlockSpec((1, planes, span, depth), lambda f: (f, 0, 0, 0)),
            pl.BlockSpec((planes, span, depth), lambda f: (0, 0, 0)),
            pl.BlockSpec((planes, span, depth), lambda f: (0, 0, 0)),
        ],
        out_specs=pl.BlockSpec((share, 1, planes - 2, span // share, depth), lambda f: (0, f, 0, 0, 0)),
        out_shape=jax.ShapeDtypeStruct((share, fields, planes - 2, span // share, depth), jnp.bfloat16),
        compiler_params=pltpu.CompilerParams(dimension_semantics=("arbitrary",)),
    )(flag, state, diffusion, velocity)


def two_steps(flag, state, before, after, diffusion, velocity, coef_before, coef_after, share):
    fields, planes, span, depth = state.shape
    halo = before.shape[1]
    field_block = lambda n: pl.BlockSpec((1, n, span, depth), lambda f: (f, 0, 0, 0))
    whole = lambda shape: pl.BlockSpec(shape, lambda f: (0,) * len(shape))
    return pl.pallas_call(
        stencil_kernel,
        grid=(fields,),
        in_specs=[
            pl.BlockSpec(memory_space=pltpu.SMEM),
            field_block(planes),
            field_block(halo),
            field_block(halo),
            whole((planes, span, depth)),
            whole((planes, span, depth)),
            whole((2, halo, span, depth)),
            whole((2, halo, span, depth)),
        ],
        out_specs=[
            field_block(planes),
            pl.BlockSpec((share, 1, 2 + planes, span // share, depth), lambda f: (0, f, 0, 0, 0)),
        ],
        out_shape=[
            jax.ShapeDtypeStruct(state.shape, jnp.float32),
            jax.ShapeDtypeStruct((share, fields, 2 + planes, span // share, depth), jnp.bfloat16),
        ],
        scratch_shapes=[pltpu.VMEM((planes + 2 * halo - 2, span, depth), jnp.float32)],
        compiler_params=pltpu.CompilerParams(dimension_semantics=("arbitrary",)),
    )(flag, state, before, after, diffusion, velocity, coef_before, coef_after)


def pieces(x):
    out, rest = [], x
    for _ in range(2):
        part = lax.reduce_precision(rest, exponent_bits=8, mantissa_bits=7)
        out.append(part.astype(jnp.bfloat16))
        rest = rest - part
    return out


def select(onehot, values):
    depth = values.shape[-1]
    parts = pieces(values)
    terms = jnp.einsum("fmk,fkd->fmd", onehot, jnp.concatenate(parts, axis=-1), preferred_element_type=jnp.float32)
    total = terms[..., :depth]
    for i in range(1, len(parts)):
        total = total + terms[..., i * depth:(i + 1) * depth]
    return total


def butterfly(value, axes):
    for axis in axes:
        n = lax.axis_size(axis)
        step = 1
        while step < n:
            value = value + lax.ppermute(value, axis, [(i, i ^ step) for i in range(n)])
            step *= 2
    return value


def work(owner, offset, profile, diffusion, velocity):
    count = lax.axis_size("space")
    fields_dev, rows_dev = offset.shape
    planes, span, depth = diffusion.shape
    cap = 4 * rows_dev // count
    slots = count * cap
    col_rows = -(-cap // depth)

    target = owner[..., 0]
    earlier = jnp.tril(jnp.ones((rows_dev, rows_dev), jnp.bool_), -1)
    same = target[:, :, None] == target[:, None, :]
    rank = jnp.sum(jnp.logical_and(same, earlier[None]), axis=2)
    slot = target * cap + rank
    hit = slot[:, None, :] == lax.broadcasted_iota(jnp.int32, (fields_dev, slots, rows_dev), 1)
    send_vals = select(hit.astype(jnp.bfloat16), profile)
    send_cols = jnp.sum(jnp.where(hit, offset[:, None, :], 0), axis=2).astype(jnp.float32)
    send_cols = jnp.pad(send_cols.reshape(fields_dev, count, cap), ((0, 0), (0, 0), (0, col_rows * depth - cap)))
    payload = jnp.concatenate(
        [send_vals.reshape(fields_dev, count, cap, depth), send_cols.reshape(fields_dev, count, col_rows, depth)],
        axis=2,
    )
    got = lax.all_to_all(payload, "space", split_axis=1, concat_axis=1, tiled=True)
    got_vals = got[:, :, :cap].reshape(fields_dev, slots, depth)
    got_cols = got[:, :, cap:].reshape(fields_dev, count, col_rows * depth)[:, :, :cap]
    got_cols = got_cols.reshape(fields_dev, slots).astype(jnp.int32)

    place = got_cols[:, None, :] == lax.broadcasted_iota(jnp.int32, (fields_dev, planes * span, slots), 1)
    state = select(place.astype(jnp.bfloat16), got_vals).reshape(fields_dev, planes, span, depth)

    adjoint = lax.axis_index("batch") >= lax.axis_size("batch") // 2
    flag = adjoint.astype(jnp.int32).reshape(1)
    coef_before, coef_after = halos_shared(jnp.stack([diffusion, velocity]), STEPS, 1)
    share = lax.axis_size("batch")
    inner = interior_step(flag, state, diffusion, velocity, share)
    before, after = halos(state, "space", STEPS, 1)
    state, late = two_steps(flag, state, before, after, diffusion, velocity, coef_before, coef_after, share)

    def spread(snap):
        mixed = lax.all_to_all(snap, "batch", split_axis=0, concat_axis=0, tiled=True)
        return mixed.reshape(mixed.shape[0] * mixed.shape[1], mixed.shape[2], -1)

    inner, late = spread(inner), spread(late)
    levels = [late[:, 0:4].reshape(late.shape[0], STEPS, 2, -1), jnp.stack([inner, late[:, 4:]], axis=1)]
    partial_gram = None
    for group in levels:
        term = jnp.einsum(
            "jtpc,iupc->tjui", group[ACT:ACT + SENS], group[:ACT], preferred_element_type=jnp.float32
        ).reshape(STEPS * SENS, STEPS * ACT)
        partial_gram = term if partial_gram is None else partial_gram + term
    scale = 4.0 / math.sqrt(planes * count * span * depth)
    gram = butterfly(partial_gram, ("batch", "space")) * scale
    return (state, gram)


def solution(mesh):
    in_specs = (
        P("batch", "space", None),
        P("batch", "space"),
        P("batch", "space", None),
        P("space", None, None),
        P("space", None, None),
    )
    out_specs = (P("batch", "space", None, None), P())
    return jax.shard_map(work, mesh=mesh, in_specs=in_specs, out_specs=out_specs, check_vma=False)
```

```python
import math

import jax
import jax.numpy as jnp
from jax import lax
from jax.experimental import pallas as pl
from jax.experimental.pallas import tpu as pltpu
from jax.sharding import PartitionSpec as P

STEPS = 2
ACT = 4
SENS = 4


LINK = jnp.bfloat16


def halos(value, axis, width, dim):
    peers, length = lax.axis_size(axis), value.shape[dim]
    up = [(i, (i + 1) % peers) for i in range(peers)]
    down = [(j, i) for i, j in up]
    last = lax.slice_in_dim(value, length - width, length, axis=dim).astype(LINK)
    initial = lax.slice_in_dim(value, 0, width, axis=dim).astype(LINK)
    return lax.ppermute(last, axis, up), lax.ppermute(initial, axis, down)


def halos_shared(value, width, dim):
    peers, pair = lax.axis_size("space"), lax.axis_size("batch")
    if pair % 2:
        return halos(value, "space", width, dim)
    length = value.shape[dim]
    odd = lax.axis_index("batch") % 2 == 1
    last = lax.slice_in_dim(value, length - width, length, axis=dim)
    initial = lax.slice_in_dim(value, 0, width, axis=dim)
    routes = []
    for s in range(peers):
        for b in range(pair):
            ahead = (s + 1) % peers if b % 2 == 0 else (s - 1) % peers
            routes.append((s * pair + b, ahead * pair + b))
    got = lax.ppermute(jnp.where(odd, initial, last).astype(LINK), ("space", "batch"), routes)
    other = lax.ppermute(got, "batch", [(b, b ^ 1) for b in range(pair)])
    return jnp.where(odd, other, got), jnp.where(odd, got, other)


ROWS = 256


def stencil_parts(flag_ref, x_ref, xb_ref, xa_ref, d_ref, v_ref, cb_ref, ca_ref, halo):
    planes, span, depth = x_ref.shape[1], x_ref.shape[2], x_ref.shape[3]
    block = math.gcd(span, ROWS)
    tiles = span // block
    sub = lax.broadcasted_iota(jnp.int32, (block, depth), 0)
    lane = lax.broadcasted_iota(jnp.int32, (block, depth), 1)

    def rows(c):
        return pl.ds(pl.multiple_of(c * block, block), block)

    def level0(k, c):
        if k < halo:
            return xb_ref[0, k, rows(c), :].astype(jnp.float32)
        if k < halo + planes:
            return x_ref[0, k - halo, rows(c), :]
        return xa_ref[0, k - halo - planes, rows(c), :].astype(jnp.float32)

    def coef(which, k, c):
        if k < halo:
            return cb_ref[which, k, rows(c), :].astype(jnp.float32)
        if k < halo + planes:
            return (d_ref if which == 0 else v_ref)[k - halo, rows(c), :]
        return ca_ref[which, k - halo - planes, rows(c), :].astype(jnp.float32)

    def lap(m, zero, p, before, after):
        total = p + m
        up = jnp.where(sub == block - 1, pltpu.roll(after, block - 1, 0), pltpu.roll(zero, block - 1, 0))
        down = jnp.where(sub == 0, pltpu.roll(before, 1, 0), pltpu.roll(zero, 1, 0))
        total = total + up + down
        zu = jnp.where(lane == depth - 1, 0.0, pltpu.roll(zero, depth - 1, 1))
        zd = jnp.where(lane == 0, 0.0, pltpu.roll(zero, 1, 1))
        total = total + zu + zd
        return total - 6.0 * zero

    def update(load, k, c, adjoint):
        prev, nxt = (c + tiles - 1) % tiles, (c + 1) % tiles
        xm, x0, xp = load(k - 1, c), load(k, c), load(k + 1, c)
        xbefore, xafter = load(k, prev), load(k, nxt)
        if adjoint:
            lifted = lap(coef(0, k - 1, c) * xm, coef(0, k, c) * x0, coef(0, k + 1, c) * xp,
                         coef(0, k, prev) * xbefore, coef(0, k, nxt) * xafter)
            slope = 0.5 * (coef(1, k + 1, c) * xp - coef(1, k - 1, c) * xm)
            return x0 + lifted + slope
        lifted = lap(xm, x0, xp, xbefore, xafter)
        slope = 0.5 * (xp - xm)
        return x0 + coef(0, k, c) * lifted - coef(1, k, c) * slope

    def store(ref, slot, c, value):
        quarter = ref.shape[3]
        per = block // quarter
        for j in range(per):
            ref[c * per + j, 0, slot] = value[j * quarter:(j + 1) * quarter].astype(ref.dtype)

    def both(run):
        @pl.when(flag_ref[0] == 0)
        def _():
            run(False)

        @pl.when(flag_ref[0] != 0)
        def _():
            run(True)

    return planes, tiles, rows, level0, update, both, store


def interior_kernel(flag_ref, x_ref, d_ref, v_ref, s_ref):
    halo = STEPS
    planes, tiles, _, level0, update, both, store = stencil_parts(
        flag_ref, x_ref, None, None, d_ref, v_ref, None, None, halo)

    def run(adjoint):
        for k in range(halo + 1, halo + planes - 1):
            def first(c, carry, k=k):
                store(s_ref, k - halo - 1, c, update(level0, k, c, adjoint))
                return carry

            lax.fori_loop(0, tiles, first, 0, unroll=2)

    both(run)


def stencil_kernel(flag_ref, x_ref, xb_ref, xa_ref, d_ref, v_ref, cb_ref, ca_ref, out_ref, late_ref, mid_ref):
    halo = xb_ref.shape[1]
    planes, tiles, rows, level0, update, both, store = stencil_parts(
        flag_ref, x_ref, xb_ref, xa_ref, d_ref, v_ref, cb_ref, ca_ref, halo)
    ext = planes + 2 * halo

    def level1(k, c):
        return mid_ref[k - 1, rows(c), :]

    def run(adjoint):
        for k in range(1, ext - 1):
            def first(c, carry, k=k):
                value = update(level0, k, c, adjoint)
                mid_ref[k - 1, rows(c), :] = value
                if k == halo or k == halo + planes - 1:
                    store(late_ref, 0 if k == halo else 1, c, value)
                return carry

            lax.fori_loop(0, tiles, first, 0, unroll=2)
        for k in range(halo, halo + planes):
            def second(c, carry, k=k):
                value = update(level1, k, c, adjoint)
                out_ref[0, k - halo, rows(c), :] = value
                p = k - halo
                store(late_ref, 2 + (0 if p == 0 else 1 if p == planes - 1 else 1 + p), c, value)
                return carry

            lax.fori_loop(0, tiles, second, 0, unroll=2)

    both(run)


def interior_step(flag, state, diffusion, velocity, share):
    fields, planes, span, depth = state.shape
    return pl.pallas_call(
        interior_kernel,
        grid=(fields,),
        in_specs=[
            pl.BlockSpec(memory_space=pltpu.SMEM),
            pl.BlockSpec((1, planes, span, depth), lambda f: (f, 0, 0, 0)),
            pl.BlockSpec((planes, span, depth), lambda f: (0, 0, 0)),
            pl.BlockSpec((planes, span, depth), lambda f: (0, 0, 0)),
        ],
        out_specs=pl.BlockSpec((share, 1, planes - 2, span // share, depth), lambda f: (0, f, 0, 0, 0)),
        out_shape=jax.ShapeDtypeStruct((share, fields, planes - 2, span // share, depth), jnp.bfloat16),
        compiler_params=pltpu.CompilerParams(dimension_semantics=("arbitrary",)),
    )(flag, state, diffusion, velocity)


def two_steps(flag, state, before, after, diffusion, velocity, coef_before, coef_after, share):
    fields, planes, span, depth = state.shape
    halo = before.shape[1]
    field_block = lambda n: pl.BlockSpec((1, n, span, depth), lambda f: (f, 0, 0, 0))
    whole = lambda shape: pl.BlockSpec(shape, lambda f: (0,) * len(shape))
    return pl.pallas_call(
        stencil_kernel,
        grid=(fields,),
        in_specs=[
            pl.BlockSpec(memory_space=pltpu.SMEM),
            field_block(planes),
            field_block(halo),
            field_block(halo),
            whole((planes, span, depth)),
            whole((planes, span, depth)),
            whole((2, halo, span, depth)),
            whole((2, halo, span, depth)),
        ],
        out_specs=[
            field_block(planes),
            pl.BlockSpec((share, 1, 2 + planes, span // share, depth), lambda f: (0, f, 0, 0, 0)),
        ],
        out_shape=[
            jax.ShapeDtypeStruct(state.shape, jnp.float32),
            jax.ShapeDtypeStruct((share, fields, 2 + planes, span // share, depth), jnp.bfloat16),
        ],
        scratch_shapes=[pltpu.VMEM((planes + 2 * halo - 2, span, depth), jnp.float32)],
        compiler_params=pltpu.CompilerParams(dimension_semantics=("arbitrary",)),
    )(flag, state, before, after, diffusion, velocity, coef_before, coef_after)


def pieces(x):
    out, rest = [], x
    for _ in range(2):
        part = lax.reduce_precision(rest, exponent_bits=8, mantissa_bits=7)
        out.append(part.astype(jnp.bfloat16))
        rest = rest - part
    return out


def select(onehot, values):
    depth = values.shape[-1]
    parts = pieces(values)
    terms = jnp.einsum("fmk,fkd->fmd", onehot, jnp.concatenate(parts, axis=-1), preferred_element_type=jnp.float32)
    total = terms[..., :depth]
    for i in range(1, len(parts)):
        total = total + terms[..., i * depth:(i + 1) * depth]
    return total


def butterfly(value, axes):
    for axis in axes:
        n = lax.axis_size(axis)
        step = 1
        while step < n:
            value = value + lax.ppermute(value, axis, [(i, i ^ step) for i in range(n)])
            step *= 2
    return value


def work(owner, offset, profile, diffusion, velocity):
    count = lax.axis_size("space")
    fields_dev, rows_dev = offset.shape
    planes, span, depth = diffusion.shape
    cap = 4 * rows_dev // count
    slots = count * cap
    col_rows = -(-cap // depth)

    target = owner[..., 0]
    earlier = jnp.tril(jnp.ones((rows_dev, rows_dev), jnp.bool_), -1)
    same = target[:, :, None] == target[:, None, :]
    rank = jnp.sum(jnp.logical_and(same, earlier[None]), axis=2)
    slot = target * cap + rank
    hit = slot[:, None, :] == lax.broadcasted_iota(jnp.int32, (fields_dev, slots, rows_dev), 1)
    send_vals = select(hit.astype(jnp.bfloat16), profile)
    send_cols = jnp.sum(jnp.where(hit, offset[:, None, :], 0), axis=2).astype(jnp.float32)
    col_rows = -(-fields_dev * cap // depth)
    send_cols = send_cols.reshape(fields_dev, count, cap).transpose(1, 0, 2).reshape(count, fields_dev * cap)
    send_cols = jnp.pad(send_cols, ((0, 0), (0, col_rows * depth - fields_dev * cap)))
    vals = send_vals.reshape(fields_dev, count, cap, depth).transpose(1, 0, 2, 3)
    payload = jnp.concatenate(
        [vals.reshape(count, fields_dev * cap, depth), send_cols.reshape(count, col_rows, depth)], axis=1
    )
    got = lax.all_to_all(payload, "space", split_axis=0, concat_axis=0, tiled=True)
    got_vals = got[:, :fields_dev * cap].reshape(count, fields_dev, cap, depth).transpose(1, 0, 2, 3)
    got_vals = got_vals.reshape(fields_dev, slots, depth)
    got_cols = got[:, fields_dev * cap:].reshape(count, col_rows * depth)[:, :fields_dev * cap]
    got_cols = got_cols.reshape(count, fields_dev, cap).transpose(1, 0, 2).reshape(fields_dev, slots).astype(jnp.int32)

    place = got_cols[:, None, :] == lax.broadcasted_iota(jnp.int32, (fields_dev, planes * span, slots), 1)
    state = select(place.astype(jnp.bfloat16), got_vals).reshape(fields_dev, planes, span, depth)

    adjoint = lax.axis_index("batch") >= lax.axis_size("batch") // 2
    flag = adjoint.astype(jnp.int32).reshape(1)
    coef_before, coef_after = halos_shared(jnp.stack([diffusion, velocity]), STEPS, 1)
    share = lax.axis_size("batch")
    inner = interior_step(flag, state, diffusion, velocity, share)
    before, after = halos(state, "space", STEPS, 1)
    state, late = two_steps(flag, state, before, after, diffusion, velocity, coef_before, coef_after, share)

    def spread(snap):
        mixed = lax.all_to_all(snap, "batch", split_axis=0, concat_axis=0, tiled=True)
        return mixed.reshape(mixed.shape[0] * mixed.shape[1], mixed.shape[2], -1)

    inner, late = spread(inner), spread(late)
    snaps = [(late[:, 0:2], inner), (late[:, 2:4], late[:, 4:])]
    rows = []
    for sensed in snaps:
        row = []
        for actuated in snaps:
            block = None
            for s_part, a_part in zip(sensed, actuated):
                term = lax.dot_general(
                    s_part[ACT:ACT + SENS].reshape(SENS, -1), a_part[:ACT].reshape(ACT, -1),
                    (((1,), (1,)), ((), ())), preferred_element_type=jnp.float32,
                )
                block = term if block is None else block + term
            row.append(block)
        rows.append(jnp.concatenate(row, axis=1))
    partial_gram = jnp.concatenate(rows, axis=0)
    scale = 4.0 / math.sqrt(planes * count * span * depth)
    gram = butterfly(partial_gram, ("batch", "space")) * scale
    return (state, gram)


def solution(mesh):
    in_specs = (
        P("batch", "space", None),
        P("batch", "space"),
        P("batch", "space", None),
        P("space", None, None),
        P("space", None, None),
    )
    out_specs = (P("batch", "space", None, None), P())
    return jax.shard_map(work, mesh=mesh, in_specs=in_specs, out_specs=out_specs, check_vma=False)
```

```python
import math

import jax
import jax.numpy as jnp
from jax import lax
from jax.experimental import pallas as pl
from jax.experimental.pallas import tpu as pltpu
from jax.sharding import PartitionSpec as P

STEPS = 2
ACT = 4
SENS = 4


LINK = jnp.bfloat16


def halos(value, axis, width, dim):
    peers, length = lax.axis_size(axis), value.shape[dim]
    up = [(i, (i + 1) % peers) for i in range(peers)]
    down = [(j, i) for i, j in up]
    last = lax.slice_in_dim(value, length - width, length, axis=dim).astype(LINK)
    initial = lax.slice_in_dim(value, 0, width, axis=dim).astype(LINK)
    return lax.ppermute(last, axis, up), lax.ppermute(initial, axis, down)


def halos_shared(value, width, dim):
    peers, pair = lax.axis_size("space"), lax.axis_size("batch")
    if pair % 2:
        return halos(value, "space", width, dim)
    length = value.shape[dim]
    odd = lax.axis_index("batch") % 2 == 1
    last = lax.slice_in_dim(value, length - width, length, axis=dim)
    initial = lax.slice_in_dim(value, 0, width, axis=dim)
    routes = []
    for s in range(peers):
        for b in range(pair):
            ahead = (s + 1) % peers if b % 2 == 0 else (s - 1) % peers
            routes.append((s * pair + b, ahead * pair + b))
    got = lax.ppermute(jnp.where(odd, initial, last).astype(LINK), ("space", "batch"), routes)
    other = lax.ppermute(got, "batch", [(b, b ^ 1) for b in range(pair)])
    return jnp.where(odd, other, got), jnp.where(odd, got, other)


ROWS = 256


def stencil_parts(flag_ref, x_ref, xb_ref, xa_ref, d_ref, v_ref, cb_ref, ca_ref, halo):
    planes, span, depth = x_ref.shape[1], x_ref.shape[2], x_ref.shape[3]
    block = math.gcd(span, ROWS)
    tiles = span // block
    sub = lax.broadcasted_iota(jnp.int32, (block, depth), 0)
    lane = lax.broadcasted_iota(jnp.int32, (block, depth), 1)

    def rows(c):
        return pl.ds(pl.multiple_of(c * block, block), block)

    def level0(k, c):
        if k < halo:
            return xb_ref[0, k, rows(c), :].astype(jnp.float32)
        if k < halo + planes:
            return x_ref[0, k - halo, rows(c), :]
        return xa_ref[0, k - halo - planes, rows(c), :].astype(jnp.float32)

    def coef(which, k, c):
        if k < halo:
            return cb_ref[which, k, rows(c), :].astype(jnp.float32)
        if k < halo + planes:
            return (d_ref if which == 0 else v_ref)[k - halo, rows(c), :]
        return ca_ref[which, k - halo - planes, rows(c), :].astype(jnp.float32)

    def lap(m, zero, p, before, after):
        total = p + m
        up = jnp.where(sub == block - 1, pltpu.roll(after, block - 1, 0), pltpu.roll(zero, block - 1, 0))
        down = jnp.where(sub == 0, pltpu.roll(before, 1, 0), pltpu.roll(zero, 1, 0))
        total = total + up + down
        zu = jnp.where(lane == depth - 1, 0.0, pltpu.roll(zero, depth - 1, 1))
        zd = jnp.where(lane == 0, 0.0, pltpu.roll(zero, 1, 1))
        total = total + zu + zd
        return total - 6.0 * zero

    def update(load, k, c, adjoint):
        prev, nxt = (c + tiles - 1) % tiles, (c + 1) % tiles
        xm, x0, xp = load(k - 1, c), load(k, c), load(k + 1, c)
        xbefore, xafter = load(k, prev), load(k, nxt)
        if adjoint:
            lifted = lap(coef(0, k - 1, c) * xm, coef(0, k, c) * x0, coef(0, k + 1, c) * xp,
                         coef(0, k, prev) * xbefore, coef(0, k, nxt) * xafter)
            slope = 0.5 * (coef(1, k + 1, c) * xp - coef(1, k - 1, c) * xm)
            return x0 + lifted + slope
        lifted = lap(xm, x0, xp, xbefore, xafter)
        slope = 0.5 * (xp - xm)
        return x0 + coef(0, k, c) * lifted - coef(1, k, c) * slope

    def store(ref, slot, c, value):
        quarter = ref.shape[3]
        per = block // quarter
        for j in range(per):
            ref[c * per + j, 0, slot] = value[j * quarter:(j + 1) * quarter].astype(ref.dtype)

    def both(run):
        @pl.when(flag_ref[0] == 0)
        def _():
            run(False)

        @pl.when(flag_ref[0] != 0)
        def _():
            run(True)

    return planes, tiles, rows, level0, update, both, store


def interior_kernel(flag_ref, x_ref, d_ref, v_ref, s_ref):
    halo = STEPS
    planes, tiles, _, level0, update, both, store = stencil_parts(
        flag_ref, x_ref, None, None, d_ref, v_ref, None, None, halo)

    def run(adjoint):
        for k in range(halo + 1, halo + planes - 1):
            def first(c, carry, k=k):
                store(s_ref, k - halo - 1, c, update(level0, k, c, adjoint))
                return carry

            lax.fori_loop(0, tiles, first, 0, unroll=2)

    both(run)


def stencil_kernel(flag_ref, x_ref, xb_ref, xa_ref, d_ref, v_ref, cb_ref, ca_ref, out_ref, late_ref, mid_ref):
    halo = xb_ref.shape[1]
    planes, tiles, rows, level0, update, both, store = stencil_parts(
        flag_ref, x_ref, xb_ref, xa_ref, d_ref, v_ref, cb_ref, ca_ref, halo)
    ext = planes + 2 * halo

    def level1(k, c):
        return mid_ref[k - 1, rows(c), :]

    def run(adjoint):
        for k in range(1, ext - 1):
            def first(c, carry, k=k):
                value = update(level0, k, c, adjoint)
                mid_ref[k - 1, rows(c), :] = value
                if k == halo or k == halo + planes - 1:
                    store(late_ref, 0 if k == halo else 1, c, value)
                return carry

            lax.fori_loop(0, tiles, first, 0, unroll=2)
        for k in range(halo, halo + planes):
            def second(c, carry, k=k):
                value = update(level1, k, c, adjoint)
                out_ref[0, k - halo, rows(c), :] = value
                p = k - halo
                store(late_ref, 2 + (0 if p == 0 else 1 if p == planes - 1 else 1 + p), c, value)
                return carry

            lax.fori_loop(0, tiles, second, 0, unroll=2)

    both(run)


def interior_step(flag, state, diffusion, velocity, share):
    fields, planes, span, depth = state.shape
    return pl.pallas_call(
        interior_kernel,
        grid=(fields,),
        in_specs=[
            pl.BlockSpec(memory_space=pltpu.SMEM),
            pl.BlockSpec((1, planes, span, depth), lambda f: (f, 0, 0, 0)),
            pl.BlockSpec((planes, span, depth), lambda f: (0, 0, 0)),
            pl.BlockSpec((planes, span, depth), lambda f: (0, 0, 0)),
        ],
        out_specs=pl.BlockSpec((share, 1, planes - 2, span // share, depth), lambda f: (0, f, 0, 0, 0)),
        out_shape=jax.ShapeDtypeStruct((share, fields, planes - 2, span // share, depth), jnp.bfloat16),
        compiler_params=pltpu.CompilerParams(dimension_semantics=("arbitrary",)),
    )(flag, state, diffusion, velocity)


def two_steps(flag, state, before, after, diffusion, velocity, coef_before, coef_after, share):
    fields, planes, span, depth = state.shape
    halo = before.shape[1]
    field_block = lambda n: pl.BlockSpec((1, n, span, depth), lambda f: (f, 0, 0, 0))
    whole = lambda shape: pl.BlockSpec(shape, lambda f: (0,) * len(shape))
    return pl.pallas_call(
        stencil_kernel,
        grid=(fields,),
        in_specs=[
            pl.BlockSpec(memory_space=pltpu.SMEM),
            field_block(planes),
            field_block(halo),
            field_block(halo),
            whole((planes, span, depth)),
            whole((planes, span, depth)),
            whole((2, halo, span, depth)),
            whole((2, halo, span, depth)),
        ],
        out_specs=[
            field_block(planes),
            pl.BlockSpec((share, 1, 2 + planes, span // share, depth), lambda f: (0, f, 0, 0, 0)),
        ],
        out_shape=[
            jax.ShapeDtypeStruct(state.shape, jnp.float32),
            jax.ShapeDtypeStruct((share, fields, 2 + planes, span // share, depth), jnp.bfloat16),
        ],
        scratch_shapes=[pltpu.VMEM((planes + 2 * halo - 2, span, depth), jnp.float32)],
        compiler_params=pltpu.CompilerParams(dimension_semantics=("arbitrary",)),
    )(flag, state, before, after, diffusion, velocity, coef_before, coef_after)


def pieces(x):
    out, rest = [], x
    for _ in range(2):
        part = lax.reduce_precision(rest, exponent_bits=8, mantissa_bits=7)
        out.append(part.astype(jnp.bfloat16))
        rest = rest - part
    return out


def select(onehot, values):
    depth = values.shape[-1]
    parts = pieces(values)
    terms = jnp.einsum("fmk,fkd->fmd", onehot, jnp.concatenate(parts, axis=-1), preferred_element_type=jnp.float32)
    total = terms[..., :depth]
    for i in range(1, len(parts)):
        total = total + terms[..., i * depth:(i + 1) * depth]
    return total


def butterfly(value, axes):
    for axis in axes:
        n = lax.axis_size(axis)
        step = 1
        while step < n:
            value = value + lax.ppermute(value, axis, [(i, i ^ step) for i in range(n)])
            step *= 2
    return value


def work(owner, offset, profile, diffusion, velocity):
    count = lax.axis_size("space")
    fields_dev, rows_dev = offset.shape
    planes, span, depth = diffusion.shape
    cap = 4 * rows_dev // count
    slots = count * cap
    col_rows = -(-cap // depth)

    target = owner[..., 0]
    earlier = jnp.tril(jnp.ones((rows_dev, rows_dev), jnp.bool_), -1)
    same = target[:, :, None] == target[:, None, :]
    rank = jnp.sum(jnp.logical_and(same, earlier[None]), axis=2)
    slot = target * cap + rank
    hit = slot[:, None, :] == lax.broadcasted_iota(jnp.int32, (fields_dev, slots, rows_dev), 1)
    send_vals = select(hit.astype(jnp.bfloat16), profile)
    send_cols = jnp.sum(jnp.where(hit, offset[:, None, :], 0), axis=2).astype(jnp.float32)
    send_cols = jnp.pad(send_cols.reshape(fields_dev, count, cap), ((0, 0), (0, 0), (0, col_rows * depth - cap)))
    payload = jnp.concatenate(
        [send_vals.reshape(fields_dev, count, cap, depth), send_cols.reshape(fields_dev, count, col_rows, depth)],
        axis=2,
    )
    got = lax.all_to_all(payload, "space", split_axis=1, concat_axis=1, tiled=True)
    got_vals = got[:, :, :cap].reshape(fields_dev, slots, depth)
    got_cols = got[:, :, cap:].reshape(fields_dev, count, col_rows * depth)[:, :, :cap]
    got_cols = got_cols.reshape(fields_dev, slots).astype(jnp.int32)

    place = got_cols[:, None, :] == lax.broadcasted_iota(jnp.int32, (fields_dev, planes * span, slots), 1)
    state = select(place.astype(jnp.bfloat16), got_vals).reshape(fields_dev, planes, span, depth)

    adjoint = lax.axis_index("batch") >= lax.axis_size("batch") // 2
    flag = adjoint.astype(jnp.int32).reshape(1)
    coef_before, coef_after = halos_shared(jnp.stack([diffusion, velocity]), STEPS, 1)
    share = lax.axis_size("batch")
    inner = interior_step(flag, state, diffusion, velocity, share)
    before, after = halos(state, "space", STEPS, 1)
    state, late = two_steps(flag, state, before, after, diffusion, velocity, coef_before, coef_after, share)

    def spread(snap):
        mixed = lax.all_to_all(snap, "batch", split_axis=0, concat_axis=0, tiled=True)
        return mixed.reshape(mixed.shape[0] * mixed.shape[1], mixed.shape[2], -1)

    inner = spread(inner)
    late = spread(late)
    snaps = [(late[:, 0:2], inner), (late[:, 2:4], late[:, 4:])]
    rows = []
    for sensed in snaps:
        row = []
        for actuated in snaps:
            block = None
            for s_part, a_part in zip(sensed, actuated):
                term = lax.dot_general(
                    s_part[ACT:ACT + SENS].reshape(SENS, -1), a_part[:ACT].reshape(ACT, -1),
                    (((1,), (1,)), ((), ())), preferred_element_type=jnp.float32,
                )
                block = term if block is None else block + term
            row.append(block)
        rows.append(jnp.concatenate(row, axis=1))
    partial_gram = jnp.concatenate(rows, axis=0)
    scale = 4.0 / math.sqrt(planes * count * span * depth)
    gram = butterfly(partial_gram, ("batch", "space")) * scale
    return (state, gram)


def solution(mesh):
    in_specs = (
        P("batch", "space", None),
        P("batch", "space"),
        P("batch", "space", None),
        P("space", None, None),
        P("space", None, None),
    )
    out_specs = (P("batch", "space", None, None), P())
    return jax.shard_map(work, mesh=mesh, in_specs=in_specs, out_specs=out_specs, check_vma=False)
```
